512 devices in a mesh: dp: 32 (over x, z_lo), tensor: 16 (over z_hi, y, core).
Axes of the slice: x: 4, y: 4, z: 16 (z_hi: 2, z_lo: 8; z = z_hi * 8 + z_lo), core: 2. Of those that a mesh axis runs over, the one named last changes fastest.
Arguments:
- tokens: bfloat16 [8192, 8192], P(('dp', 'tensor')), may hold values from -6 to 6
- norm_gain: float32 [8192], replicated, may hold values from 0.1 to 1.9
- w_query: bfloat16 [8192, 4096], P('dp', 'tensor'), may hold values from -0.0625 to 0.0625
- w_key: bfloat16 [8192, 512], P('dp', 'tensor'), may hold values from -0.0625 to 0.0625
- w_value: bfloat16 [8192, 512], P('dp', 'tensor'), may hold values from -0.0625 to 0.0625
- w_out: bfloat16 [4096, 8192], P('tensor', 'dp'), may hold values from -0.25 to 0.25
Outputs:
- layer_out: bfloat16 [8192, 8192], P(('dp', 'tensor'))
The draws below stay inside these ranges and needn't reach their ends.
All inputs are finite; a program needn't handle non-finite values.
Results may differ from the reference program's by a relative error of at most 0.019.
Values may be sent and summed in bfloat16 or wider, within the bound.
No kernel may reach another device: no remote copies, remote signals or barrier semaphores. Data moves between devices by JAX's collectives and lax.ppermute only.
A program may use at most 64 MiB of HBM per device.

```python
import math
import jax
import jax.numpy as jnp
from jax import lax

D = 8192
QH = 32
KVH = 4
HD = 128
SEQ = 128
TOKENS = 8192
N_TENSOR = 16


def steps_of(own_key, dims, shards, least, high):
    factor_of = 1.0
    for dim, parts in shards:
        draws = jax.random.uniform(jax.random.fold_in(jax.random.fold_in(own_key, 6), dim), (parts,), jnp.float32, least / len(shards), high / len(shards))
        factor_of = factor_of * jnp.repeat(jnp.exp(draws), dims[dim] // parts).reshape((-1,) + (1,) * (len(dims) - 1 - dim))
    return factor_of


def bell_draw(stream_key, dims, spread, bound, split=(), held_as=jnp.bfloat16):
    loudness = steps_of(stream_key, dims, split, -0.22, 0.18) if split else 1.0
    entries = jax.random.normal(stream_key, dims, jnp.float32) * spread * loudness
    return jnp.minimum(jnp.maximum(entries, -bound), bound).astype(held_as)


def setup_inputs(seed: int = 0) -> dict:
    seeds = jax.random.split(jax.random.key(seed), 7)
    return {
        "tokens": bell_draw(seeds[0], (TOKENS, D), 1.0, 6.0, ((0, 512),)),
        "norm_gain": jnp.clip(1.0 + 0.18 * jax.random.normal(seeds[1], (D,), jnp.float32), 0.1, 1.9),
        "w_query": bell_draw(seeds[2], (D, QH * HD), D ** -0.5, 0.0625, ((0, 32), (1, 16))),
        "w_key": bell_draw(seeds[3], (D, KVH * HD), D ** -0.5, 0.0625, ((0, 32), (1, 16))),
        "w_value": bell_draw(seeds[4], (D, KVH * HD), D ** -0.5, 0.0625, ((0, 32), (1, 16))),
        "w_out": bell_draw(seeds[5], (QH * HD, D), (HD * 4) ** -0.5, 0.25, ((0, 16), (1, 32))),
    }


theta_base = 500000.0
epsilon = 1e-05

def normalize(tokens, norm_gain):
    widened = tokens.astype(jnp.float32)
    mean_square = lax.optimization_barrier(jnp.mean(widened * widened, axis=-1, keepdims=True))
    return (widened * lax.rsqrt(mean_square + epsilon) * norm_gain[None, :]).astype(jnp.bfloat16)

def head_major(matrix, head_count):
    row_count = matrix.shape[0]
    head_width = matrix.shape[1] // head_count
    return jnp.transpose(matrix.reshape(row_count, head_width, head_count), (0, 2, 1)).reshape(row_count, head_count * head_width)

def rotary(matrix, head_count, seq_span):
    row_count = matrix.shape[0]
    head_width = matrix.shape[1] // head_count
    half_width = head_width // 2
    position = (jnp.arange(row_count, dtype=jnp.int32) % seq_span).astype(jnp.float32)
    frequency = jnp.exp(jnp.arange(half_width, dtype=jnp.float32) * (-2.0 * math.log(theta_base) / head_width))
    angles = position[:, None] * frequency[None, :]
    cosine = jnp.cos(angles)[:, None, :]
    sine_part = jnp.sin(angles)[:, None, :]
    shaped = matrix.reshape(row_count, head_count, head_width)
    first_half = shaped[..., :half_width]
    second_half = shaped[..., half_width:]
    joined = jnp.concatenate([first_half * cosine - second_half * sine_part, second_half * cosine + first_half * sine_part], axis=-1)
    return joined.reshape(row_count, head_count * head_width)

def attend(queries, key_heads, value_heads, seq_span):
    row_count, head_count, head_width = queries.shape
    seq_count = row_count // seq_span
    query_four = queries.reshape(seq_count, seq_span, head_count, head_width).astype(jnp.float32)
    key_four = key_heads.reshape(seq_count, seq_span, head_count, head_width).astype(jnp.float32)
    value_four = value_heads.reshape(seq_count, seq_span, head_count, head_width).astype(jnp.float32)
    scores = jnp.einsum('nqhd,nkhd->nhqk', query_four, key_four) * (1.0 / math.sqrt(head_width))
    causal = jnp.arange(seq_span)[:, None] >= jnp.arange(seq_span)[None, :]
    raw_weights = jnp.where(causal[None, None], jnp.exp(scores), 0.0)
    weights = (raw_weights / lax.optimization_barrier(jnp.sum(raw_weights, axis=-1, keepdims=True))).astype(jnp.bfloat16)
    attended = jnp.einsum('nhqk,nkhd->nqhd', weights.astype(jnp.float32), value_four)
    return attended.astype(jnp.bfloat16).reshape(row_count, head_count * head_width)

def reference(tokens, norm_gain, w_query, w_key, w_value, w_out):
    normed = normalize(tokens, norm_gain)
    row_count = tokens.shape[0]
    queries = rotary(jnp.dot(normed, w_query, preferred_element_type=jnp.float32), QH, SEQ).astype(jnp.bfloat16)
    keys = rotary(head_major(jnp.dot(normed, w_key, preferred_element_type=jnp.float32), KVH), KVH, SEQ).astype(jnp.bfloat16)
    values = head_major(jnp.dot(normed, w_value, preferred_element_type=jnp.float32), KVH).astype(jnp.bfloat16)

    def expand_heads(matrix):
        return jnp.repeat(matrix.reshape(row_count, KVH, HD), QH // KVH, axis=1)
    mixed = attend(queries.reshape(row_count, QH, HD), expand_heads(keys), expand_heads(values), SEQ)
    group_cols = QH * HD // N_TENSOR
    branch = jnp.zeros((row_count, D), jnp.float32)
    for group_index in range(N_TENSOR):
        lower = group_index * group_cols
        group_part = jnp.dot(mixed[:, lower:lower + group_cols], w_out[lower:lower + group_cols], preferred_element_type=jnp.float32)
        rounded = lax.optimization_barrier(group_part.astype(jnp.bfloat16))
        branch = branch + rounded.astype(jnp.float32)
    return (tokens.astype(jnp.float32) + branch).astype(jnp.bfloat16)
```

```python
import math

import jax
import jax.numpy as jnp
from jax import lax
from jax.sharding import Mesh, PartitionSpec as P

QH = 32
KVH = 4
HD = 128
SEQ = 128


theta_base = 500000.0
epsilon = 1e-05


def normalize(tokens, norm_gain):
    widened = tokens.astype(jnp.float32)
    mean_square = jnp.mean(widened * widened, axis=-1, keepdims=True)
    return (widened * lax.rsqrt(mean_square + epsilon) * norm_gain[None, :]).astype(jnp.bfloat16)


def head_major(matrix, head_count):
    row_count = matrix.shape[0]
    head_width = matrix.shape[1] // head_count
    return jnp.transpose(matrix.reshape(row_count, head_width, head_count), (0, 2, 1)).reshape(
        row_count, head_count * head_width
    )


def rotary(matrix, head_count, seq_span):
    row_count = matrix.shape[0]
    head_width = matrix.shape[1] // head_count
    half_width = head_width // 2
    position = (jnp.arange(row_count, dtype=jnp.int32) % seq_span).astype(jnp.float32)
    frequency = jnp.exp(
        jnp.arange(half_width, dtype=jnp.float32) * (-2.0 * math.log(theta_base) / head_width)
    )
    angles = position[:, None] * frequency[None, :]
    cosine = jnp.cos(angles)[:, None, :]
    sine_part = jnp.sin(angles)[:, None, :]
    shaped = matrix.reshape(row_count, head_count, head_width)
    first_half = shaped[..., :half_width]
    second_half = shaped[..., half_width:]
    joined = jnp.concatenate(
        [
            first_half * cosine - second_half * sine_part,
            second_half * cosine + first_half * sine_part,
        ],
        axis=-1,
    )
    return joined.reshape(row_count, head_count * head_width)


def attend(queries, key_heads, value_heads, seq_span):
    row_count, head_count, head_width = queries.shape
    seq_count = row_count // seq_span
    query_four = queries.reshape(seq_count, seq_span, head_count, head_width)
    key_four = key_heads.reshape(seq_count, seq_span, head_count, head_width)
    value_four = value_heads.reshape(seq_count, seq_span, head_count, head_width)
    scores = jnp.einsum(
        "nqhd,nkhd->nhqk", query_four, key_four, preferred_element_type=jnp.float32
    ) * (1.0 / math.sqrt(head_width))
    causal = jnp.arange(seq_span)[:, None] >= jnp.arange(seq_span)[None, :]
    raw_weights = jnp.where(causal[None, None], jnp.exp(scores), 0.0)
    weights = (raw_weights / jnp.sum(raw_weights, axis=-1, keepdims=True)).astype(jnp.bfloat16)
    attended = jnp.einsum(
        "nhqk,nkhd->nqhd", weights, value_four, preferred_element_type=jnp.float32
    )
    return attended.astype(jnp.bfloat16).reshape(row_count, head_count * head_width)


def ring_gather(block, axis_name, size):
    if size == 1:
        return block[None]
    index = lax.axis_index(axis_name)
    forward = [(s, (s + 1) % size) for s in range(size)]
    backward = [(s, (s - 1) % size) for s in range(size)]
    relative = [None] * size
    relative[0] = block
    ahead = block
    behind = block
    for step in range(1, size // 2 + 1):
        ahead = lax.ppermute(ahead, axis_name, forward)
        relative[(-step) % size] = ahead
        if step < size - size // 2:
            behind = lax.ppermute(behind, axis_name, backward)
            relative[step] = behind
    stacked = jnp.stack(relative)
    return jnp.roll(stacked, index, axis=0)


def group_gather(block):
    along_y = ring_gather(block, "y", 4)
    along_zh = ring_gather(along_y, "zh", 2)
    along_c = ring_gather(along_zh, "c", 2)
    ordered = jnp.moveaxis(along_c, 0, 2)
    return ordered.reshape((-1,) + block.shape[1:])


def dp_gather(block, axis):
    return lax.all_gather(lax.all_gather(block, "zl", axis=axis, tiled=True), "x", axis=axis, tiled=True)


def body(tokens, norm_gain, w_query, w_key, w_value, w_out):
    tensor_rank = (lax.axis_index("zh") * 4 + lax.axis_index("y")) * 2 + lax.axis_index("c")
    normed = normalize(tokens, norm_gain)
    gathered = group_gather(normed)
    row_count = gathered.shape[0]
    q_cols = w_query.shape[1]
    k_cols = w_key.shape[1]
    weights = dp_gather(jnp.concatenate([w_query, w_key, w_value], axis=1), 0)
    projected = jnp.dot(gathered, weights, preferred_element_type=jnp.float32)
    query_part = projected[:, :q_cols]
    kv_part = projected[:, q_cols:].astype(jnp.bfloat16)
    kv_all = group_gather(kv_part.T)
    kv_all = kv_all.reshape(-1, 2, k_cols, row_count)
    key_whole = jnp.transpose(kv_all[:, 0], (2, 0, 1)).reshape(row_count, -1).astype(jnp.float32)
    value_whole = jnp.transpose(kv_all[:, 1], (2, 0, 1)).reshape(row_count, -1).astype(jnp.float32)
    local_heads = q_cols // HD
    queries = (
        rotary(query_part, local_heads, SEQ)
        .astype(jnp.bfloat16)
        .reshape(row_count, local_heads, HD)
    )
    key_heads = (
        rotary(head_major(key_whole, KVH), KVH, SEQ)
        .astype(jnp.bfloat16)
        .reshape(row_count, KVH, HD)
    )
    value_heads = head_major(value_whole, KVH).astype(jnp.bfloat16).reshape(row_count, KVH, HD)
    owner = (tensor_rank * local_heads + jnp.arange(local_heads, dtype=jnp.int32)) // (QH // KVH)
    key_heads = jnp.take(key_heads, owner, axis=1)
    value_heads = jnp.take(value_heads, owner, axis=1)
    mixed = attend(queries, key_heads, value_heads, SEQ)
    partial_out = jnp.dot(
        mixed, dp_gather(w_out, 1), preferred_element_type=jnp.float32
    ).astype(jnp.bfloat16)
    width = partial_out.shape[1]
    regrouped = partial_out.reshape(2, -1, row_count // 16, width).transpose(1, 0, 2, 3)
    regrouped = regrouped.reshape(row_count, width)
    summed = lax.psum_scatter(regrouped, ("y", "c"), scatter_dimension=0, tiled=True)
    summed = lax.psum_scatter(summed, "zh", scatter_dimension=0, tiled=True).astype(jnp.float32)
    return (tokens.astype(jnp.float32) + summed).astype(jnp.bfloat16)


def solution(mesh):
    fine = Mesh(mesh.devices.reshape(4, 8, 2, 4, 2), ("x", "zl", "zh", "y", "c"))
    dp = ("x", "zl")
    tensor = ("zh", "y", "c")
    in_specs = (
        P(dp + tensor, None),
        P(),
        P(dp, tensor),
        P(dp, tensor),
        P(dp, tensor),
        P(tensor, dp),
    )
    out_specs = P(dp + tensor, None)
    return jax.shard_map(body, mesh=fine, in_specs=in_specs, out_specs=out_specs, check_vma=False)
```

```python
import math

import jax
import jax.numpy as jnp
from jax import lax
from jax.sharding import Mesh, PartitionSpec as P

QH = 32
KVH = 4
HD = 128
SEQ = 128


theta_base = 500000.0
epsilon = 1e-05


def normalize(tokens, norm_gain):
    widened = tokens.astype(jnp.float32)
    mean_square = jnp.mean(widened * widened, axis=-1, keepdims=True)
    return (widened * lax.rsqrt(mean_square + epsilon) * norm_gain[None, :]).astype(jnp.bfloat16)


def head_major(matrix, head_count):
    row_count = matrix.shape[0]
    head_width = matrix.shape[1] // head_count
    return jnp.transpose(matrix.reshape(row_count, head_width, head_count), (0, 2, 1)).reshape(
        row_count, head_count * head_width
    )


def rotary(matrix, head_count, seq_span):
    row_count = matrix.shape[0]
    head_width = matrix.shape[1] // head_count
    half_width = head_width // 2
    position = (jnp.arange(row_count, dtype=jnp.int32) % seq_span).astype(jnp.float32)
    frequency = jnp.exp(
        jnp.arange(half_width, dtype=jnp.float32) * (-2.0 * math.log(theta_base) / head_width)
    )
    angles = position[:, None] * frequency[None, :]
    cosine = jnp.cos(angles)[:, None, :]
    sine_part = jnp.sin(angles)[:, None, :]
    shaped = matrix.reshape(row_count, head_count, head_width)
    first_half = shaped[..., :half_width]
    second_half = shaped[..., half_width:]
    joined = jnp.concatenate(
        [
            first_half * cosine - second_half * sine_part,
            second_half * cosine + first_half * sine_part,
        ],
        axis=-1,
    )
    return joined.reshape(row_count, head_count * head_width)


def attend(queries, key_heads, value_heads, seq_span):
    row_count, head_count, head_width = queries.shape
    seq_count = row_count // seq_span
    query_four = queries.reshape(seq_count, seq_span, head_count, head_width)
    key_four = key_heads.reshape(seq_count, seq_span, head_count, head_width)
    value_four = value_heads.reshape(seq_count, seq_span, head_count, head_width)
    scores = jnp.einsum(
        "nqhd,nkhd->nhqk", query_four, key_four, preferred_element_type=jnp.float32
    ) * (1.0 / math.sqrt(head_width))
    causal = jnp.arange(seq_span)[:, None] >= jnp.arange(seq_span)[None, :]
    raw_weights = jnp.where(causal[None, None], jnp.exp(scores), 0.0)
    weights = (raw_weights / jnp.sum(raw_weights, axis=-1, keepdims=True)).astype(jnp.bfloat16)
    attended = jnp.einsum(
        "nhqk,nkhd->nqhd", weights, value_four, preferred_element_type=jnp.float32
    )
    return attended.astype(jnp.bfloat16).reshape(row_count, head_count * head_width)


def ring_gather(block, axis_name, size):
    if size == 1:
        return block[None]
    index = lax.axis_index(axis_name)
    forward = [(s, (s + 1) % size) for s in range(size)]
    backward = [(s, (s - 1) % size) for s in range(size)]
    relative = [None] * size
    relative[0] = block
    ahead = block
    behind = block
    for step in range(1, size // 2 + 1):
        ahead = lax.ppermute(ahead, axis_name, forward)
        relative[(-step) % size] = ahead
        if step < size - size // 2:
            behind = lax.ppermute(behind, axis_name, backward)
            relative[step] = behind
    stacked = jnp.stack(relative)
    return jnp.roll(stacked, index, axis=0)


def group_gather(block):
    along_zh = ring_gather(block, "zh", 2)
    along_y = ring_gather(along_zh, "y", 4)
    along_c = ring_gather(along_y, "c", 2)
    ordered = jnp.transpose(along_c, (2, 1, 0) + tuple(range(3, along_c.ndim)))
    return ordered.reshape((-1,) + block.shape[1:])


def dp_gather(block, axis):
    return lax.all_gather(lax.all_gather(block, "zl", axis=axis, tiled=True), "x", axis=axis, tiled=True)


def body(tokens, norm_gain, w_query, w_key, w_value, w_out):
    tensor_rank = (lax.axis_index("zh") * 4 + lax.axis_index("y")) * 2 + lax.axis_index("c")
    normed = normalize(tokens, norm_gain)
    gathered = group_gather(normed)
    row_count = gathered.shape[0]
    q_cols = w_query.shape[1]
    k_cols = w_key.shape[1]
    weights = dp_gather(jnp.concatenate([w_query, w_key, w_value], axis=1), 0)
    weights, w_out = lax.optimization_barrier((weights, w_out))
    projected = jnp.dot(gathered, weights, preferred_element_type=jnp.float32)
    query_part = projected[:, :q_cols]
    kv_part = projected[:, q_cols:].astype(jnp.bfloat16)
    kv_all = group_gather(kv_part.T)
    kv_all = kv_all.reshape(-1, 2, k_cols, row_count)
    key_whole = jnp.transpose(kv_all[:, 0], (2, 0, 1)).reshape(row_count, -1).astype(jnp.float32)
    value_whole = jnp.transpose(kv_all[:, 1], (2, 0, 1)).reshape(row_count, -1).astype(jnp.float32)
    local_heads = q_cols // HD
    queries = (
        rotary(query_part, local_heads, SEQ)
        .astype(jnp.bfloat16)
        .reshape(row_count, local_heads, HD)
    )
    key_heads = (
        rotary(head_major(key_whole, KVH), KVH, SEQ)
        .astype(jnp.bfloat16)
        .reshape(row_count, KVH, HD)
    )
    value_heads = head_major(value_whole, KVH).astype(jnp.bfloat16).reshape(row_count, KVH, HD)
    owner = (tensor_rank * local_heads + jnp.arange(local_heads, dtype=jnp.int32)) // (QH // KVH)
    key_heads = jnp.take(key_heads, owner, axis=1)
    value_heads = jnp.take(value_heads, owner, axis=1)
    mixed = attend(queries, key_heads, value_heads, SEQ)
    partial_out = jnp.dot(
        mixed, dp_gather(w_out, 1), preferred_element_type=jnp.float32
    ).astype(jnp.bfloat16)
    width = partial_out.shape[1]
    regrouped = partial_out.reshape(2, -1, row_count // 16, width).transpose(1, 0, 2, 3)
    regrouped = regrouped.reshape(row_count, width)
    summed = lax.psum_scatter(regrouped, ("y", "c"), scatter_dimension=0, tiled=True)
    summed = lax.psum_scatter(summed, "zh", scatter_dimension=0, tiled=True).astype(jnp.float32)
    return (tokens.astype(jnp.float32) + summed).astype(jnp.bfloat16)


def solution(mesh):
    fine = Mesh(mesh.devices.reshape(4, 8, 2, 4, 2), ("x", "zl", "zh", "y", "c"))
    dp = ("x", "zl")
    tensor = ("zh", "y", "c")
    in_specs = (
        P(dp + tensor, None),
        P(),
        P(dp, tensor),
        P(dp, tensor),
        P(dp, tensor),
        P(tensor, dp),
    )
    out_specs = P(dp + tensor, None)
    return jax.shard_map(body, mesh=fine, in_specs=in_specs, out_specs=out_specs, check_vma=False)
```

```python
import math

import jax
import jax.numpy as jnp
from jax import lax
from jax.sharding import Mesh, PartitionSpec as P

QH = 32
KVH = 4
HD = 128
SEQ = 128


theta_base = 500000.0
epsilon = 1e-05


def normalize(tokens, norm_gain):
    widened = tokens.astype(jnp.float32)
    mean_square = jnp.mean(widened * widened, axis=-1, keepdims=True)
    return (widened * lax.rsqrt(mean_square + epsilon) * norm_gain[None, :]).astype(jnp.bfloat16)


def head_major(matrix, head_count):
    row_count = matrix.shape[0]
    head_width = matrix.shape[1] // head_count
    return jnp.transpose(matrix.reshape(row_count, head_width, head_count), (0, 2, 1)).reshape(
        row_count, head_count * head_width
    )


def rotary(matrix, head_count, seq_span):
    row_count = matrix.shape[0]
    head_width = matrix.shape[1] // head_count
    half_width = head_width // 2
    position = (jnp.arange(row_count, dtype=jnp.int32) % seq_span).astype(jnp.float32)
    frequency = jnp.exp(
        jnp.arange(half_width, dtype=jnp.float32) * (-2.0 * math.log(theta_base) / head_width)
    )
    angles = position[:, None] * frequency[None, :]
    cosine = jnp.cos(angles)[:, None, :]
    sine_part = jnp.sin(angles)[:, None, :]
    shaped = matrix.reshape(row_count, head_count, head_width)
    first_half = shaped[..., :half_width]
    second_half = shaped[..., half_width:]
    joined = jnp.concatenate(
        [
            first_half * cosine - second_half * sine_part,
            second_half * cosine + first_half * sine_part,
        ],
        axis=-1,
    )
    return joined.reshape(row_count, head_count * head_width)


def attend(queries, key_heads, value_heads, seq_span):
    row_count, head_count, head_width = queries.shape
    seq_count = row_count // seq_span
    query_four = queries.reshape(seq_count, seq_span, head_count, head_width)
    key_four = key_heads.reshape(seq_count, seq_span, head_count, head_width)
    value_four = value_heads.reshape(seq_count, seq_span, head_count, head_width)
    scores = jnp.einsum(
        "nqhd,nkhd->nhqk", query_four, key_four, preferred_element_type=jnp.float32
    ) * (1.0 / math.sqrt(head_width))
    causal = jnp.arange(seq_span)[:, None] >= jnp.arange(seq_span)[None, :]
    raw_weights = jnp.where(causal[None, None], jnp.exp(scores), 0.0)
    weights = (raw_weights / jnp.sum(raw_weights, axis=-1, keepdims=True)).astype(jnp.bfloat16)
    attended = jnp.einsum(
        "nhqk,nkhd->nqhd", weights, value_four, preferred_element_type=jnp.float32
    )
    return attended.astype(jnp.bfloat16).reshape(row_count, head_count * head_width)


def ring_gather(block, axis_name, size):
    if size == 1:
        return block[None]
    index = lax.axis_index(axis_name)
    forward = [(s, (s + 1) % size) for s in range(size)]
    backward = [(s, (s - 1) % size) for s in range(size)]
    relative = [None] * size
    relative[0] = block
    ahead = block
    behind = block
    for step in range(1, size // 2 + 1):
        ahead = lax.ppermute(ahead, axis_name, forward)
        relative[(-step) % size] = ahead
        if step < size - size // 2:
            behind = lax.ppermute(behind, axis_name, backward)
            relative[step] = behind
    stacked = jnp.stack(relative)
    return jnp.roll(stacked, index, axis=0)


def group_gather(block):
    along_zh = ring_gather(block, "zh", 2)
    along_y = ring_gather(along_zh, "y", 4)
    along_c = ring_gather(along_y, "c", 2)
    ordered = jnp.transpose(along_c, (2, 1, 0) + tuple(range(3, along_c.ndim)))
    return ordered.reshape((-1,) + block.shape[1:])


def dp_gather(block):
    along_x = ring_gather(block, "x", 4)
    return lax.all_gather(along_x, "zl", axis=1)


def take(array, index, axis):
    return lax.dynamic_index_in_dim(array, index, axis=axis, keepdims=False)


def group_reduce_scatter(partial):
    c_index = lax.axis_index("c")
    y_index = lax.axis_index("y")
    zh_index = lax.axis_index("zh")
    swap = [(0, 1), (1, 0)]
    sent = lax.ppermute(take(partial, 1 - c_index, 2), "c", swap)
    acc = take(partial, c_index, 2).astype(jnp.float32) + sent.astype(jnp.float32)
    mine = take(acc, y_index, 1)
    for shift in range(1, 4):
        outgoing = take(acc, (y_index + shift) % 4, 1).astype(jnp.bfloat16)
        mine = mine + lax.ppermute(outgoing, "y", [(s, (s + shift) % 4) for s in range(4)]).astype(jnp.float32)
    sent = lax.ppermute(take(mine, 1 - zh_index, 0).astype(jnp.bfloat16), "zh", swap)
    return take(mine, zh_index, 0) + sent.astype(jnp.float32)


def body(tokens, norm_gain, w_query, w_key, w_value, w_out):
    tensor_rank = (lax.axis_index("zh") * 4 + lax.axis_index("y")) * 2 + lax.axis_index("c")
    normed = normalize(tokens, norm_gain)
    gathered = group_gather(normed)
    row_count = gathered.shape[0]
    q_cols = w_query.shape[1]
    k_cols = w_key.shape[1]
    weights = dp_gather(jnp.concatenate([w_query, w_key, w_value], axis=1))
    weights = weights.reshape(-1, weights.shape[-1])
    weights, w_out = lax.optimization_barrier((weights, w_out))
    projected = jnp.dot(gathered, weights, preferred_element_type=jnp.float32)
    query_part = projected[:, :q_cols]
    kv_part = projected[:, q_cols:].astype(jnp.bfloat16)
    kv_all = group_gather(kv_part.T)
    kv_all = kv_all.reshape(-1, 2, k_cols, row_count)
    key_whole = jnp.transpose(kv_all[:, 0], (2, 0, 1)).reshape(row_count, -1).astype(jnp.float32)
    value_whole = jnp.transpose(kv_all[:, 1], (2, 0, 1)).reshape(row_count, -1).astype(jnp.float32)
    local_heads = q_cols // HD
    queries = (
        rotary(query_part, local_heads, SEQ)
        .astype(jnp.bfloat16)
        .reshape(row_count, local_heads, HD)
    )
    key_heads = (
        rotary(head_major(key_whole, KVH), KVH, SEQ)
        .astype(jnp.bfloat16)
        .reshape(row_count, KVH, HD)
    )
    value_heads = head_major(value_whole, KVH).astype(jnp.bfloat16).reshape(row_count, KVH, HD)
    owner = (tensor_rank * local_heads + jnp.arange(local_heads, dtype=jnp.int32)) // (QH // KVH)
    key_heads = jnp.take(key_heads, owner, axis=1)
    value_heads = jnp.take(value_heads, owner, axis=1)
    mixed = attend(queries, key_heads, value_heads, SEQ)
    out_weights = dp_gather(w_out)
    partial_out = jnp.einsum(
        "rk,xzkc->rxzc", mixed, out_weights, preferred_element_type=jnp.float32
    ).astype(jnp.bfloat16)
    width = partial_out.shape[1] * partial_out.shape[2] * partial_out.shape[3]
    summed = group_reduce_scatter(partial_out.reshape(2, 4, 2, row_count // 16, width))
    return (tokens.astype(jnp.float32) + summed).astype(jnp.bfloat16)


def solution(mesh):
    fine = Mesh(mesh.devices.reshape(4, 8, 2, 4, 2), ("x", "zl", "zh", "y", "c"))
    dp = ("x", "zl")
    tensor = ("zh", "y", "c")
    in_specs = (
        P(dp + tensor, None),
        P(),
        P(dp, tensor),
        P(dp, tensor),
        P(dp, tensor),
        P(tensor, dp),
    )
    out_specs = P(dp + tensor, None)
    return jax.shard_map(body, mesh=fine, in_specs=in_specs, out_specs=out_specs, check_vma=False)
```

```python
import math

import jax
import jax.numpy as jnp
from jax import lax
from jax.sharding import Mesh, PartitionSpec as P

QH = 32
KVH = 4
HD = 128
SEQ = 128


theta_base = 500000.0
epsilon = 1e-05


def normalize(tokens, norm_gain):
    widened = tokens.astype(jnp.float32)
    mean_square = jnp.mean(widened * widened, axis=-1, keepdims=True)
    return (widened * lax.rsqrt(mean_square + epsilon) * norm_gain[None, :]).astype(jnp.bfloat16)


def head_major(matrix, head_count):
    row_count = matrix.shape[0]
    head_width = matrix.shape[1] // head_count
    return jnp.transpose(matrix.reshape(row_count, head_width, head_count), (0, 2, 1)).reshape(
        row_count, head_count * head_width
    )


def rotary(matrix, head_count, seq_span):
    row_count = matrix.shape[0]
    head_width = matrix.shape[1] // head_count
    half_width = head_width // 2
    position = (jnp.arange(row_count, dtype=jnp.int32) % seq_span).astype(jnp.float32)
    frequency = jnp.exp(
        jnp.arange(half_width, dtype=jnp.float32) * (-2.0 * math.log(theta_base) / head_width)
    )
    angles = position[:, None] * frequency[None, :]
    cosine = jnp.cos(angles)[:, None, :]
    sine_part = jnp.sin(angles)[:, None, :]
    shaped = matrix.reshape(row_count, head_count, head_width)
    first_half = shaped[..., :half_width]
    second_half = shaped[..., half_width:]
    joined = jnp.concatenate(
        [
            first_half * cosine - second_half * sine_part,
            second_half * cosine + first_half * sine_part,
        ],
        axis=-1,
    )
    return joined.reshape(row_count, head_count * head_width)


def attend(queries, key_heads, value_heads, seq_span):
    row_count, head_count, head_width = queries.shape
    seq_count = row_count // seq_span
    query_four = queries.reshape(seq_count, seq_span, head_count, head_width)
    key_four = key_heads.reshape(seq_count, seq_span, head_count, head_width)
    value_four = value_heads.reshape(seq_count, seq_span, head_count, head_width)
    scores = jnp.einsum(
        "nqhd,nkhd->nhqk", query_four, key_four, preferred_element_type=jnp.float32
    ) * (1.0 / math.sqrt(head_width))
    causal = jnp.arange(seq_span)[:, None] >= jnp.arange(seq_span)[None, :]
    raw_weights = jnp.where(causal[None, None], jnp.exp(scores), 0.0)
    weights = (raw_weights / jnp.sum(raw_weights, axis=-1, keepdims=True)).astype(jnp.bfloat16)
    attended = jnp.einsum(
        "nhqk,nkhd->nqhd", weights, value_four, preferred_element_type=jnp.float32
    )
    return attended.astype(jnp.bfloat16).reshape(row_count, head_count * head_width)


def ring_gather(block, axis_name, size):
    if size == 1:
        return block[None]
    index = lax.axis_index(axis_name)
    forward = [(s, (s + 1) % size) for s in range(size)]
    backward = [(s, (s - 1) % size) for s in range(size)]
    relative = [None] * size
    relative[0] = block
    ahead = block
    behind = block
    for step in range(1, size // 2 + 1):
        ahead = lax.ppermute(ahead, axis_name, forward)
        relative[(-step) % size] = ahead
        if step < size - size // 2:
            behind = lax.ppermute(behind, axis_name, backward)
            relative[step] = behind
    stacked = jnp.stack(relative)
    return jnp.roll(stacked, index, axis=0)


def group_gather(block):
    along_zh = ring_gather(block, "zh", 2)
    along_y = ring_gather(along_zh, "y", 4)
    along_c = ring_gather(along_y, "c", 2)
    ordered = jnp.transpose(along_c, (2, 1, 0) + tuple(range(3, along_c.ndim)))
    return ordered.reshape((-1,) + block.shape[1:])


def dp_gather(block, axis):
    return lax.all_gather(lax.all_gather(block, "zl", axis=axis, tiled=True), "x", axis=axis, tiled=True)


def take(array, index, axis):
    return lax.dynamic_index_in_dim(array, index, axis=axis, keepdims=False)


def group_reduce_scatter(partial):
    c_index = lax.axis_index("c")
    y_index = lax.axis_index("y")
    zh_index = lax.axis_index("zh")
    swap = [(0, 1), (1, 0)]
    sent = lax.ppermute(take(partial, 1 - c_index, 2), "c", swap)
    acc = take(partial, c_index, 2).astype(jnp.float32) + sent.astype(jnp.float32)
    mine = take(acc, y_index, 1)
    for shift in range(1, 4):
        outgoing = take(acc, (y_index + shift) % 4, 1).astype(jnp.bfloat16)
        mine = mine + lax.ppermute(outgoing, "y", [(s, (s + shift) % 4) for s in range(4)]).astype(jnp.float32)
    sent = lax.ppermute(take(mine, 1 - zh_index, 0).astype(jnp.bfloat16), "zh", swap)
    return take(mine, zh_index, 0) + sent.astype(jnp.float32)


def body(tokens, norm_gain, w_query, w_key, w_value, w_out):
    tensor_rank = (lax.axis_index("zh") * 4 + lax.axis_index("y")) * 2 + lax.axis_index("c")
    q_cols = w_query.shape[1]
    k_cols = w_key.shape[1]
    stacked = jnp.concatenate([w_query, w_key, w_value], axis=1)
    normed = normalize(tokens, norm_gain)
    stacked, normed = lax.optimization_barrier((stacked, normed))
    weights = dp_gather(stacked, 0)
    gathered = group_gather(normed)
    row_count = gathered.shape[0]
    weights, w_out = lax.optimization_barrier((weights, w_out))
    projected = jnp.dot(gathered, weights, preferred_element_type=jnp.float32)
    query_part = projected[:, :q_cols]
    kv_part = projected[:, q_cols:].astype(jnp.bfloat16)
    kv_all = group_gather(kv_part.T)
    kv_all = kv_all.reshape(-1, 2, k_cols, row_count)
    key_whole = jnp.transpose(kv_all[:, 0], (2, 0, 1)).reshape(row_count, -1).astype(jnp.float32)
    value_whole = jnp.transpose(kv_all[:, 1], (2, 0, 1)).reshape(row_count, -1).astype(jnp.float32)
    local_heads = q_cols // HD
    queries = (
        rotary(query_part, local_heads, SEQ)
        .astype(jnp.bfloat16)
        .reshape(row_count, local_heads, HD)
    )
    key_heads = (
        rotary(head_major(key_whole, KVH), KVH, SEQ)
        .astype(jnp.bfloat16)
        .reshape(row_count, KVH, HD)
    )
    value_heads = head_major(value_whole, KVH).astype(jnp.bfloat16).reshape(row_count, KVH, HD)
    owner = (tensor_rank * local_heads + jnp.arange(local_heads, dtype=jnp.int32)) // (QH // KVH)
    key_heads = jnp.take(key_heads, owner, axis=1)
    value_heads = jnp.take(value_heads, owner, axis=1)
    mixed = attend(queries, key_heads, value_heads, SEQ)
    partial_out = jnp.dot(
        mixed, dp_gather(w_out, 1), preferred_element_type=jnp.float32
    ).astype(jnp.bfloat16)
    width = partial_out.shape[1]
    summed = group_reduce_scatter(partial_out.reshape(2, 4, 2, row_count // 16, width))
    return (tokens.astype(jnp.float32) + summed).astype(jnp.bfloat16)


def solution(mesh):
    fine = Mesh(mesh.devices.reshape(4, 8, 2, 4, 2), ("x", "zl", "zh", "y", "c"))
    dp = ("x", "zl")
    tensor = ("zh", "y", "c")
    in_specs = (
        P(dp + tensor, None),
        P(),
        P(dp, tensor),
        P(dp, tensor),
        P(dp, tensor),
        P(tensor, dp),
    )
    out_specs = P(dp + tensor, None)
    return jax.shard_map(body, mesh=fine, in_specs=in_specs, out_specs=out_specs, check_vma=False)
```

```python
import math

import jax
import jax.numpy as jnp
from jax import lax
from jax.sharding import Mesh, PartitionSpec as P

QH = 32
KVH = 4
HD = 128
SEQ = 128


theta_base = 500000.0
epsilon = 1e-05


def normalize(tokens, norm_gain):
    widened = tokens.astype(jnp.float32)
    mean_square = jnp.mean(widened * widened, axis=-1, keepdims=True)
    return (widened * lax.rsqrt(mean_square + epsilon) * norm_gain[None, :]).astype(jnp.bfloat16)


def head_major(matrix, head_count):
    row_count = matrix.shape[0]
    head_width = matrix.shape[1] // head_count
    return jnp.transpose(matrix.reshape(row_count, head_width, head_count), (0, 2, 1)).reshape(
        row_count, head_count * head_width
    )


def rotary(matrix, head_count, seq_span):
    row_count = matrix.shape[0]
    head_width = matrix.shape[1] // head_count
    half_width = head_width // 2
    position = (jnp.arange(row_count, dtype=jnp.int32) % seq_span).astype(jnp.float32)
    frequency = jnp.exp(
        jnp.arange(half_width, dtype=jnp.float32) * (-2.0 * math.log(theta_base) / head_width)
    )
    angles = position[:, None] * frequency[None, :]
    cosine = jnp.cos(angles)[:, None, :]
    sine_part = jnp.sin(angles)[:, None, :]
    shaped = matrix.reshape(row_count, head_count, head_width)
    first_half = shaped[..., :half_width]
    second_half = shaped[..., half_width:]
    joined = jnp.concatenate(
        [
            first_half * cosine - second_half * sine_part,
            second_half * cosine + first_half * sine_part,
        ],
        axis=-1,
    )
    return joined.reshape(row_count, head_count * head_width)


def attend(queries, key_heads, value_heads, seq_span):
    row_count, head_count, head_width = queries.shape
    seq_count = row_count // seq_span
    query_four = queries.reshape(seq_count, seq_span, head_count, head_width)
    key_four = key_heads.reshape(seq_count, seq_span, head_count, head_width)
    value_four = value_heads.reshape(seq_count, seq_span, head_count, head_width)
    scores = jnp.einsum(
        "nqhd,nkhd->nhqk", query_four, key_four, preferred_element_type=jnp.float32
    ) * (1.0 / math.sqrt(head_width))
    causal = jnp.arange(seq_span)[:, None] >= jnp.arange(seq_span)[None, :]
    raw_weights = jnp.where(causal[None, None], jnp.exp(scores), 0.0)
    weights = (raw_weights / jnp.sum(raw_weights, axis=-1, keepdims=True)).astype(jnp.bfloat16)
    attended = jnp.einsum(
        "nhqk,nkhd->nqhd", weights, value_four, preferred_element_type=jnp.float32
    )
    return attended.astype(jnp.bfloat16).reshape(row_count, head_count * head_width)


def ring_gather(block, axis_name, size):
    if size == 1:
        return block[None]
    index = lax.axis_index(axis_name)
    forward = [(s, (s + 1) % size) for s in range(size)]
    backward = [(s, (s - 1) % size) for s in range(size)]
    relative = [None] * size
    relative[0] = block
    ahead = block
    behind = block
    for step in range(1, size // 2 + 1):
        ahead = lax.ppermute(ahead, axis_name, forward)
        relative[(-step) % size] = ahead
        if step < size - size // 2:
            behind = lax.ppermute(behind, axis_name, backward)
            relative[step] = behind
    stacked = jnp.stack(relative)
    return jnp.roll(stacked, index, axis=0)


def group_gather(block):
    along_zh = ring_gather(block, "zh", 2)
    along_y = ring_gather(along_zh, "y", 4)
    along_c = ring_gather(along_y, "c", 2)
    ordered = jnp.transpose(along_c, (2, 1, 0) + tuple(range(3, along_c.ndim)))
    return ordered.reshape((-1,) + block.shape[1:])


def dp_gather(block, axis):
    return lax.all_gather(lax.all_gather(block, "zl", axis=axis, tiled=True), "x", axis=axis, tiled=True)


def take(array, index, axis):
    return lax.dynamic_index_in_dim(array, index, axis=axis, keepdims=False)


def group_reduce_scatter(partial):
    c_index = lax.axis_index("c")
    y_index = lax.axis_index("y")
    zh_index = lax.axis_index("zh")
    swap = [(0, 1), (1, 0)]
    sent = lax.ppermute(take(partial, 1 - c_index, 2), "c", swap)
    acc = take(partial, c_index, 2).astype(jnp.float32) + sent.astype(jnp.float32)
    mine = take(acc, y_index, 1)
    for shift in range(1, 4):
        outgoing = take(acc, (y_index + shift) % 4, 1).astype(jnp.bfloat16)
        mine = mine + lax.ppermute(outgoing, "y", [(s, (s + shift) % 4) for s in range(4)]).astype(jnp.float32)
    sent = lax.ppermute(take(mine, 1 - zh_index, 0).astype(jnp.bfloat16), "zh", swap)
    return take(mine, zh_index, 0) + sent.astype(jnp.float32)


def body(tokens, norm_gain, w_query, w_key, w_value, w_out):
    tensor_rank = (lax.axis_index("zh") * 4 + lax.axis_index("y")) * 2 + lax.axis_index("c")
    q_cols = w_query.shape[1]
    k_cols = w_key.shape[1]
    stacked = jnp.concatenate([w_query, w_key, w_value], axis=1)
    normed = normalize(tokens, norm_gain)
    stacked, normed = lax.optimization_barrier((stacked, normed))
    payload = jnp.concatenate([stacked.reshape(-1), w_out.reshape(-1)])
    along_zl = lax.all_gather(payload, "zl", axis=0)
    in_part = along_zl[:, : stacked.size].reshape(-1, stacked.shape[1])
    out_part = along_zl[:, stacked.size :].reshape((-1,) + w_out.shape)
    weights = lax.all_gather(in_part, "x", axis=0, tiled=True)
    weights, out_part = lax.optimization_barrier((weights, out_part))
    out_part = jnp.transpose(out_part, (1, 0, 2)).reshape(w_out.shape[0], -1)
    out_weights = lax.all_gather(out_part, "x", axis=1, tiled=True)
    gathered = group_gather(normed)
    row_count = gathered.shape[0]
    projected = jnp.dot(gathered, weights, preferred_element_type=jnp.float32)
    query_part = projected[:, :q_cols]
    kv_part = projected[:, q_cols:].astype(jnp.bfloat16)
    kv_all = group_gather(kv_part.T)
    kv_all = kv_all.reshape(-1, 2, k_cols, row_count)
    key_whole = jnp.transpose(kv_all[:, 0], (2, 0, 1)).reshape(row_count, -1).astype(jnp.float32)
    value_whole = jnp.transpose(kv_all[:, 1], (2, 0, 1)).reshape(row_count, -1).astype(jnp.float32)
    local_heads = q_cols // HD
    queries = (
        rotary(query_part, local_heads, SEQ)
        .astype(jnp.bfloat16)
        .reshape(row_count, local_heads, HD)
    )
    key_heads = (
        rotary(head_major(key_whole, KVH), KVH, SEQ)
        .astype(jnp.bfloat16)
        .reshape(row_count, KVH, HD)
    )
    value_heads = head_major(value_whole, KVH).astype(jnp.bfloat16).reshape(row_count, KVH, HD)
    owner = (tensor_rank * local_heads + jnp.arange(local_heads, dtype=jnp.int32)) // (QH // KVH)
    key_heads = jnp.take(key_heads, owner, axis=1)
    value_heads = jnp.take(value_heads, owner, axis=1)
    mixed = attend(queries, key_heads, value_heads, SEQ)
    partial_out = jnp.dot(
        mixed, out_weights, preferred_element_type=jnp.float32
    ).astype(jnp.bfloat16)
    width = partial_out.shape[1]
    summed = group_reduce_scatter(partial_out.reshape(2, 4, 2, row_count // 16, width))
    return (tokens.astype(jnp.float32) + summed).astype(jnp.bfloat16)


def solution(mesh):
    fine = Mesh(mesh.devices.reshape(4, 8, 2, 4, 2), ("x", "zl", "zh", "y", "c"))
    dp = ("x", "zl")
    tensor = ("zh", "y", "c")
    in_specs = (
        P(dp + tensor, None),
        P(),
        P(dp, tensor),
        P(dp, tensor),
        P(dp, tensor),
        P(tensor, dp),
    )
    out_specs = P(dp + tensor, None)
    return jax.shard_map(body, mesh=fine, in_specs=in_specs, out_specs=out_specs, check_vma=False)
```

```python
import math

import jax
import jax.numpy as jnp
from jax import lax
from jax.sharding import Mesh, PartitionSpec as P

QH = 32
KVH = 4
HD = 128
SEQ = 128


theta_base = 500000.0
epsilon = 1e-05


def normalize(tokens, norm_gain):
    widened = tokens.astype(jnp.float32)
    mean_square = jnp.mean(widened * widened, axis=-1, keepdims=True)
    return (widened * lax.rsqrt(mean_square + epsilon) * norm_gain[None, :]).astype(jnp.bfloat16)


def head_major(matrix, head_count):
    row_count = matrix.shape[0]
    head_width = matrix.shape[1] // head_count
    return jnp.transpose(matrix.reshape(row_count, head_width, head_count), (0, 2, 1)).reshape(
        row_count, head_count * head_width
    )


def rotary(matrix, head_count, seq_span):
    row_count = matrix.shape[0]
    head_width = matrix.shape[1] // head_count
    half_width = head_width // 2
    position = (jnp.arange(row_count, dtype=jnp.int32) % seq_span).astype(jnp.float32)
    frequency = jnp.exp(
        jnp.arange(half_width, dtype=jnp.float32) * (-2.0 * math.log(theta_base) / head_width)
    )
    angles = position[:, None] * frequency[None, :]
    cosine = jnp.cos(angles)[:, None, :]
    sine_part = jnp.sin(angles)[:, None, :]
    shaped = matrix.reshape(row_count, head_count, head_width)
    first_half = shaped[..., :half_width]
    second_half = shaped[..., half_width:]
    joined = jnp.concatenate(
        [
            first_half * cosine - second_half * sine_part,
            second_half * cosine + first_half * sine_part,
        ],
        axis=-1,
    )
    return joined.reshape(row_count, head_count * head_width)


def attend(queries, key_heads, value_heads, seq_span):
    row_count, head_count, head_width = queries.shape
    seq_count = row_count // seq_span
    query_four = queries.reshape(seq_count, seq_span, head_count, head_width)
    key_four = key_heads.reshape(seq_count, seq_span, head_count, head_width)
    value_four = value_heads.reshape(seq_count, seq_span, head_count, head_width)
    scores = jnp.einsum(
        "nqhd,nkhd->nhqk", query_four, key_four, preferred_element_type=jnp.float32
    ) * (1.0 / math.sqrt(head_width))
    causal = jnp.arange(seq_span)[:, None] >= jnp.arange(seq_span)[None, :]
    raw_weights = jnp.where(causal[None, None], jnp.exp(scores), 0.0)
    weights = (raw_weights / jnp.sum(raw_weights, axis=-1, keepdims=True)).astype(jnp.bfloat16)
    attended = jnp.einsum(
        "nhqk,nkhd->nqhd", weights, value_four, preferred_element_type=jnp.float32
    )
    return attended.astype(jnp.bfloat16).reshape(row_count, head_count * head_width)


def ring_gather(block, axis_name, size):
    if size == 1:
        return block[None]
    index = lax.axis_index(axis_name)
    forward = [(s, (s + 1) % size) for s in range(size)]
    backward = [(s, (s - 1) % size) for s in range(size)]
    relative = [None] * size
    relative[0] = block
    ahead = block
    behind = block
    for step in range(1, size // 2 + 1):
        ahead = lax.ppermute(ahead, axis_name, forward)
        relative[(-step) % size] = ahead
        if step < size - size // 2:
            behind = lax.ppermute(behind, axis_name, backward)
            relative[step] = behind
    stacked = jnp.stack(relative)
    return jnp.roll(stacked, index, axis=0)


def group_gather(block):
    along_zh = ring_gather(block, "zh", 2)
    along_y = ring_gather(along_zh, "y", 4)
    along_c = ring_gather(along_y, "c", 2)
    ordered = jnp.transpose(along_c, (2, 1, 0) + tuple(range(3, along_c.ndim)))
    return ordered.reshape((-1,) + block.shape[1:])


def dp_gather(block, axis):
    return lax.all_gather(lax.all_gather(block, "zl", axis=axis, tiled=True), "x", axis=axis, tiled=True)


def take(array, index, axis):
    return lax.dynamic_index_in_dim(array, index, axis=axis, keepdims=False)


def group_reduce_scatter(partial):
    c_index = lax.axis_index("c")
    y_index = lax.axis_index("y")
    zh_index = lax.axis_index("zh")
    swap = [(0, 1), (1, 0)]
    sent = lax.ppermute(take(partial, 1 - c_index, 2), "c", swap)
    acc = take(partial, c_index, 2).astype(jnp.float32) + sent.astype(jnp.float32)
    mine = take(acc, y_index, 1)
    for shift in range(1, 4):
        outgoing = take(acc, (y_index + shift) % 4, 1).astype(jnp.bfloat16)
        mine = mine + lax.ppermute(outgoing, "y", [(s, (s + shift) % 4) for s in range(4)]).astype(jnp.float32)
    sent = lax.ppermute(take(mine, 1 - zh_index, 0).astype(jnp.bfloat16), "zh", swap)
    return take(mine, zh_index, 0) + sent.astype(jnp.float32)


def body(tokens, norm_gain, w_query, w_key, w_value, w_out):
    tensor_rank = (lax.axis_index("zh") * 4 + lax.axis_index("y")) * 2 + lax.axis_index("c")
    q_cols = w_query.shape[1]
    k_cols = w_key.shape[1]
    stacked = jnp.concatenate([w_query, w_key, w_value], axis=1)
    normed = normalize(tokens, norm_gain)
    stacked, normed = lax.optimization_barrier((stacked, normed))
    payload = jnp.concatenate([stacked.reshape(-1), w_out.reshape(-1)])
    along_zl = lax.all_gather(payload, "zl", axis=0)
    along_zl, normed = lax.optimization_barrier((along_zl, normed))
    in_part = along_zl[:, : stacked.size].reshape(-1, stacked.shape[1])
    out_part = along_zl[:, stacked.size :].reshape((-1,) + w_out.shape)
    weights = lax.all_gather(in_part, "x", axis=0, tiled=True)
    weights, out_part = lax.optimization_barrier((weights, out_part))
    out_part = jnp.transpose(out_part, (1, 0, 2)).reshape(w_out.shape[0], -1)
    out_weights = lax.all_gather(out_part, "x", axis=1, tiled=True)
    gathered = group_gather(normed)
    row_count = gathered.shape[0]
    projected = jnp.dot(gathered, weights, preferred_element_type=jnp.float32)
    query_part = projected[:, :q_cols]
    kv_part = projected[:, q_cols:].astype(jnp.bfloat16)
    kv_all = group_gather(kv_part.T)
    kv_all = kv_all.reshape(-1, 2, k_cols, row_count)
    key_whole = jnp.transpose(kv_all[:, 0], (2, 0, 1)).reshape(row_count, -1).astype(jnp.float32)
    value_whole = jnp.transpose(kv_all[:, 1], (2, 0, 1)).reshape(row_count, -1).astype(jnp.float32)
    local_heads = q_cols // HD
    queries = (
        rotary(query_part, local_heads, SEQ)
        .astype(jnp.bfloat16)
        .reshape(row_count, local_heads, HD)
    )
    key_heads = (
        rotary(head_major(key_whole, KVH), KVH, SEQ)
        .astype(jnp.bfloat16)
        .reshape(row_count, KVH, HD)
    )
    value_heads = head_major(value_whole, KVH).astype(jnp.bfloat16).reshape(row_count, KVH, HD)
    owner = (tensor_rank * local_heads + jnp.arange(local_heads, dtype=jnp.int32)) // (QH // KVH)
    key_heads = jnp.take(key_heads, owner, axis=1)
    value_heads = jnp.take(value_heads, owner, axis=1)
    mixed = attend(queries, key_heads, value_heads, SEQ)
    partial_out = jnp.dot(
        mixed, out_weights, preferred_element_type=jnp.float32
    ).astype(jnp.bfloat16)
    width = partial_out.shape[1]
    summed = group_reduce_scatter(partial_out.reshape(2, 4, 2, row_count // 16, width))
    return (tokens.astype(jnp.float32) + summed).astype(jnp.bfloat16)


def solution(mesh):
    fine = Mesh(mesh.devices.reshape(4, 8, 2, 4, 2), ("x", "zl", "zh", "y", "c"))
    dp = ("x", "zl")
    tensor = ("zh", "y", "c")
    in_specs = (
        P(dp + tensor, None),
        P(),
        P(dp, tensor),
        P(dp, tensor),
        P(dp, tensor),
        P(tensor, dp),
    )
    out_specs = P(dp + tensor, None)
    return jax.shard_map(body, mesh=fine, in_specs=in_specs, out_specs=out_specs, check_vma=False)
```

```python
import math

import jax
import jax.numpy as jnp
from jax import lax
from jax.sharding import Mesh, PartitionSpec as P

QH = 32
KVH = 4
HD = 128
SEQ = 128


theta_base = 500000.0
epsilon = 1e-05


def normalize(tokens, norm_gain):
    widened = tokens.astype(jnp.float32)
    mean_square = jnp.mean(widened * widened, axis=-1, keepdims=True)
    return (widened * lax.rsqrt(mean_square + epsilon) * norm_gain[None, :]).astype(jnp.bfloat16)


def head_major(matrix, head_count):
    row_count = matrix.shape[0]
    head_width = matrix.shape[1] // head_count
    return jnp.transpose(matrix.reshape(row_count, head_width, head_count), (0, 2, 1)).reshape(
        row_count, head_count * head_width
    )


def rotary(matrix, head_count, seq_span):
    row_count = matrix.shape[0]
    head_width = matrix.shape[1] // head_count
    half_width = head_width // 2
    position = (jnp.arange(row_count, dtype=jnp.int32) % seq_span).astype(jnp.float32)
    frequency = jnp.exp(
        jnp.arange(half_width, dtype=jnp.float32) * (-2.0 * math.log(theta_base) / head_width)
    )
    angles = position[:, None] * frequency[None, :]
    cosine = jnp.cos(angles)[:, None, :]
    sine_part = jnp.sin(angles)[:, None, :]
    shaped = matrix.reshape(row_count, head_count, head_width)
    first_half = shaped[..., :half_width]
    second_half = shaped[..., half_width:]
    joined = jnp.concatenate(
        [
            first_half * cosine - second_half * sine_part,
            second_half * cosine + first_half * sine_part,
        ],
        axis=-1,
    )
    return joined.reshape(row_count, head_count * head_width)


def attend(queries, key_heads, value_heads, seq_span):
    row_count, head_count, head_width = queries.shape
    seq_count = row_count // seq_span
    query_four = queries.reshape(seq_count, seq_span, head_count, head_width)
    key_four = key_heads.reshape(seq_count, seq_span, head_count, head_width)
    value_four = value_heads.reshape(seq_count, seq_span, head_count, head_width)
    scores = jnp.einsum(
        "nqhd,nkhd->nhqk", query_four, key_four, preferred_element_type=jnp.float32
    ) * (1.0 / math.sqrt(head_width))
    causal = jnp.arange(seq_span)[:, None] >= jnp.arange(seq_span)[None, :]
    raw_weights = jnp.where(causal[None, None], jnp.exp(scores), 0.0)
    weights = (raw_weights / jnp.sum(raw_weights, axis=-1, keepdims=True)).astype(jnp.bfloat16)
    attended = jnp.einsum(
        "nhqk,nkhd->nqhd", weights, value_four, preferred_element_type=jnp.float32
    )
    return attended.astype(jnp.bfloat16).reshape(row_count, head_count * head_width)


def ring_gather(block, axis_name, size):
    if size == 1:
        return block[None]
    index = lax.axis_index(axis_name)
    forward = [(s, (s + 1) % size) for s in range(size)]
    backward = [(s, (s - 1) % size) for s in range(size)]
    relative = [None] * size
    relative[0] = block
    ahead = block
    behind = block
    for step in range(1, size // 2 + 1):
        ahead = lax.ppermute(ahead, axis_name, forward)
        relative[(-step) % size] = ahead
        if step < size - size // 2:
            behind = lax.ppermute(behind, axis_name, backward)
            relative[step] = behind
    stacked = jnp.stack(relative)
    return jnp.roll(stacked, index, axis=0)


def group_gather(block):
    along_zh = ring_gather(block, "zh", 2)
    along_y = ring_gather(along_zh, "y", 4)
    along_c = ring_gather(along_y, "c", 2)
    ordered = jnp.transpose(along_c, (2, 1, 0) + tuple(range(3, along_c.ndim)))
    return ordered.reshape((-1,) + block.shape[1:])


def dp_gather(block, axis):
    return lax.all_gather(lax.all_gather(block, "zl", axis=axis, tiled=True), "x", axis=axis, tiled=True)


def take(array, index, axis):
    return lax.dynamic_index_in_dim(array, index, axis=axis, keepdims=False)


def group_reduce_scatter(partial):
    c_index = lax.axis_index("c")
    y_index = lax.axis_index("y")
    zh_index = lax.axis_index("zh")
    swap = [(0, 1), (1, 0)]
    sent = lax.ppermute(take(partial, 1 - c_index, 2), "c", swap)
    acc = take(partial, c_index, 2).astype(jnp.float32) + sent.astype(jnp.float32)
    mine = take(acc, y_index, 1)
    for shift in range(1, 4):
        outgoing = take(acc, (y_index + shift) % 4, 1).astype(jnp.bfloat16)
        mine = mine + lax.ppermute(outgoing, "y", [(s, (s + shift) % 4) for s in range(4)]).astype(jnp.float32)
    sent = lax.ppermute(take(mine, 1 - zh_index, 0).astype(jnp.bfloat16), "zh", swap)
    return take(mine, zh_index, 0) + sent.astype(jnp.float32)


def body(tokens, norm_gain, w_query, w_key, w_value, w_out):
    tensor_rank = (lax.axis_index("zh") * 4 + lax.axis_index("y")) * 2 + lax.axis_index("c")
    q_cols = w_query.shape[1]
    k_cols = w_key.shape[1]
    stacked = jnp.concatenate([w_query, w_key, w_value], axis=1)
    normed = normalize(tokens, norm_gain)
    stacked, normed = lax.optimization_barrier((stacked, normed))
    payload = jnp.concatenate([stacked, w_out], axis=1)
    along_zl = lax.all_gather(payload, "zl", axis=0, tiled=True)
    in_part = along_zl[:, : stacked.shape[1]]
    out_part = along_zl[:, stacked.shape[1] :].reshape((-1,) + w_out.shape)
    out_part = jnp.transpose(out_part, (1, 0, 2)).reshape(w_out.shape[0], -1)
    in_part, out_part, normed = lax.optimization_barrier((in_part, out_part, normed))
    weights = ring_gather(in_part, "x", 4).reshape(-1, in_part.shape[1])
    out_weights = lax.all_gather(out_part, "x", axis=1, tiled=True)
    gathered = group_gather(normed)
    row_count = gathered.shape[0]
    projected = jnp.dot(gathered, weights, preferred_element_type=jnp.float32)
    query_part = projected[:, :q_cols]
    kv_part = projected[:, q_cols:].astype(jnp.bfloat16)
    kv_all = group_gather(kv_part.T)
    kv_all = kv_all.reshape(-1, 2, k_cols, row_count)
    key_whole = jnp.transpose(kv_all[:, 0], (2, 0, 1)).reshape(row_count, -1).astype(jnp.float32)
    value_whole = jnp.transpose(kv_all[:, 1], (2, 0, 1)).reshape(row_count, -1).astype(jnp.float32)
    local_heads = q_cols // HD
    queries = (
        rotary(query_part, local_heads, SEQ)
        .astype(jnp.bfloat16)
        .reshape(row_count, local_heads, HD)
    )
    key_heads = (
        rotary(head_major(key_whole, KVH), KVH, SEQ)
        .astype(jnp.bfloat16)
        .reshape(row_count, KVH, HD)
    )
    value_heads = head_major(value_whole, KVH).astype(jnp.bfloat16).reshape(row_count, KVH, HD)
    owner = (tensor_rank * local_heads + jnp.arange(local_heads, dtype=jnp.int32)) // (QH // KVH)
    key_heads = jnp.take(key_heads, owner, axis=1)
    value_heads = jnp.take(value_heads, owner, axis=1)
    mixed = attend(queries, key_heads, value_heads, SEQ)
    partial_out = jnp.dot(
        mixed, out_weights, preferred_element_type=jnp.float32
    ).astype(jnp.bfloat16)
    width = partial_out.shape[1]
    summed = group_reduce_scatter(partial_out.reshape(2, 4, 2, row_count // 16, width))
    return (tokens.astype(jnp.float32) + summed).astype(jnp.bfloat16)


def solution(mesh):
    fine = Mesh(mesh.devices.reshape(4, 8, 2, 4, 2), ("x", "zl", "zh", "y", "c"))
    dp = ("x", "zl")
    tensor = ("zh", "y", "c")
    in_specs = (
        P(dp + tensor, None),
        P(),
        P(dp, tensor),
        P(dp, tensor),
        P(dp, tensor),
        P(tensor, dp),
    )
    out_specs = P(dp + tensor, None)
    return jax.shard_map(body, mesh=fine, in_specs=in_specs, out_specs=out_specs, check_vma=False)
```

```python
import math

import jax
import jax.numpy as jnp
from jax import lax
from jax.sharding import Mesh, PartitionSpec as P

QH = 32
KVH = 4
HD = 128
SEQ = 128


theta_base = 500000.0
epsilon = 1e-05


def normalize(tokens, norm_gain):
    widened = tokens.astype(jnp.float32)
    mean_square = jnp.mean(widened * widened, axis=-1, keepdims=True)
    return (widened * lax.rsqrt(mean_square + epsilon) * norm_gain[None, :]).astype(jnp.bfloat16)


def head_major(matrix, head_count):
    row_count = matrix.shape[0]
    head_width = matrix.shape[1] // head_count
    return jnp.transpose(matrix.reshape(row_count, head_width, head_count), (0, 2, 1)).reshape(
        row_count, head_count * head_width
    )


def rotary(matrix, head_count, seq_span):
    row_count = matrix.shape[0]
    head_width = matrix.shape[1] // head_count
    half_width = head_width // 2
    position = (jnp.arange(row_count, dtype=jnp.int32) % seq_span).astype(jnp.float32)
    frequency = jnp.exp(
        jnp.arange(half_width, dtype=jnp.float32) * (-2.0 * math.log(theta_base) / head_width)
    )
    angles = position[:, None] * frequency[None, :]
    cosine = jnp.cos(angles)[:, None, :]
    sine_part = jnp.sin(angles)[:, None, :]
    shaped = matrix.reshape(row_count, head_count, head_width)
    first_half = shaped[..., :half_width]
    second_half = shaped[..., half_width:]
    joined = jnp.concatenate(
        [
            first_half * cosine - second_half * sine_part,
            second_half * cosine + first_half * sine_part,
        ],
        axis=-1,
    )
    return joined.reshape(row_count, head_count * head_width)


def attend(queries, key_heads, value_heads, seq_span):
    row_count, head_count, head_width = queries.shape
    seq_count = row_count // seq_span
    query_four = queries.reshape(seq_count, seq_span, head_count, head_width)
    key_four = key_heads.reshape(seq_count, seq_span, head_count, head_width)
    value_four = value_heads.reshape(seq_count, seq_span, head_count, head_width)
    scores = jnp.einsum(
        "nqhd,nkhd->nhqk", query_four, key_four, preferred_element_type=jnp.float32
    ) * (1.0 / math.sqrt(head_width))
    causal = jnp.arange(seq_span)[:, None] >= jnp.arange(seq_span)[None, :]
    raw_weights = jnp.where(causal[None, None], jnp.exp(scores), 0.0)
    weights = (raw_weights / jnp.sum(raw_weights, axis=-1, keepdims=True)).astype(jnp.bfloat16)
    attended = jnp.einsum(
        "nhqk,nkhd->nqhd", weights, value_four, preferred_element_type=jnp.float32
    )
    return attended.astype(jnp.bfloat16).reshape(row_count, head_count * head_width)


def ring_gather(block, axis_name, size):
    if size == 1:
        return block[None]
    index = lax.axis_index(axis_name)
    forward = [(s, (s + 1) % size) for s in range(size)]
    backward = [(s, (s - 1) % size) for s in range(size)]
    relative = [None] * size
    relative[0] = block
    ahead = block
    behind = block
    for step in range(1, size // 2 + 1):
        ahead = lax.ppermute(ahead, axis_name, forward)
        relative[(-step) % size] = ahead
        if step < size - size // 2:
            behind = lax.ppermute(behind, axis_name, backward)
            relative[step] = behind
    stacked = jnp.stack(relative)
    return jnp.roll(stacked, index, axis=0)


def group_gather(block):
    along_zh = ring_gather(block, "zh", 2)
    along_y = ring_gather(along_zh, "y", 4)
    along_c = ring_gather(along_y, "c", 2)
    ordered = jnp.transpose(along_c, (2, 1, 0) + tuple(range(3, along_c.ndim)))
    return ordered.reshape((-1,) + block.shape[1:])


def dp_gather(block, axis):
    return lax.all_gather(lax.all_gather(block, "zl", axis=axis, tiled=True), "x", axis=axis, tiled=True)


def take(array, index, axis):
    return lax.dynamic_index_in_dim(array, index, axis=axis, keepdims=False)


def group_reduce_scatter(partial):
    c_index = lax.axis_index("c")
    y_index = lax.axis_index("y")
    zh_index = lax.axis_index("zh")
    swap = [(0, 1), (1, 0)]
    sent = lax.ppermute(take(partial, 1 - c_index, 2), "c", swap)
    acc = take(partial, c_index, 2).astype(jnp.float32) + sent.astype(jnp.float32)
    mine = take(acc, y_index, 1)
    for shift in range(1, 4):
        outgoing = take(acc, (y_index + shift) % 4, 1).astype(jnp.bfloat16)
        mine = mine + lax.ppermute(outgoing, "y", [(s, (s + shift) % 4) for s in range(4)]).astype(jnp.float32)
    sent = lax.ppermute(take(mine, 1 - zh_index, 0).astype(jnp.bfloat16), "zh", swap)
    return take(mine, zh_index, 0) + sent.astype(jnp.float32)


def body(tokens, norm_gain, w_query, w_key, w_value, w_out):
    tensor_rank = (lax.axis_index("zh") * 4 + lax.axis_index("y")) * 2 + lax.axis_index("c")
    q_cols = w_query.shape[1]
    k_cols = w_key.shape[1]
    stacked = jnp.concatenate([w_query, w_key, w_value], axis=1)
    normed = normalize(tokens, norm_gain)
    stacked, normed = lax.optimization_barrier((stacked, normed))
    payload = jnp.concatenate([stacked, w_out], axis=1)
    along_zl = lax.all_gather(payload, "zl", axis=0, tiled=True)
    in_part = along_zl[:, : stacked.shape[1]]
    out_part = along_zl[:, stacked.shape[1] :].reshape((-1,) + w_out.shape)
    out_part = jnp.transpose(out_part, (1, 0, 2)).reshape(w_out.shape[0], -1)
    in_part, out_part, normed = lax.optimization_barrier((in_part, out_part, normed))
    weights = lax.all_gather(in_part, "x", axis=0, tiled=True)
    weights, out_part = lax.optimization_barrier((weights, out_part))
    out_weights = lax.all_gather(out_part, "x", axis=1, tiled=True)
    gathered = group_gather(normed)
    row_count = gathered.shape[0]
    projected = jnp.dot(gathered, weights, preferred_element_type=jnp.float32)
    query_part = projected[:, :q_cols]
    kv_part = projected[:, q_cols:].astype(jnp.bfloat16)
    kv_all = group_gather(kv_part.T)
    kv_all = kv_all.reshape(-1, 2, k_cols, row_count)
    key_whole = jnp.transpose(kv_all[:, 0], (2, 0, 1)).reshape(row_count, -1).astype(jnp.float32)
    value_whole = jnp.transpose(kv_all[:, 1], (2, 0, 1)).reshape(row_count, -1).astype(jnp.float32)
    local_heads = q_cols // HD
    queries = (
        rotary(query_part, local_heads, SEQ)
        .astype(jnp.bfloat16)
        .reshape(row_count, local_heads, HD)
    )
    key_heads = (
        rotary(head_major(key_whole, KVH), KVH, SEQ)
        .astype(jnp.bfloat16)
        .reshape(row_count, KVH, HD)
    )
    value_heads = head_major(value_whole, KVH).astype(jnp.bfloat16).reshape(row_count, KVH, HD)
    owner = (tensor_rank * local_heads + jnp.arange(local_heads, dtype=jnp.int32)) // (QH // KVH)
    key_heads = jnp.take(key_heads, owner, axis=1)
    value_heads = jnp.take(value_heads, owner, axis=1)
    mixed = attend(queries, key_heads, value_heads, SEQ)
    partial_out = jnp.dot(
        mixed, out_weights, preferred_element_type=jnp.float32
    ).astype(jnp.bfloat16)
    width = partial_out.shape[1]
    summed = group_reduce_scatter(partial_out.reshape(2, 4, 2, row_count // 16, width))
    return (tokens.astype(jnp.float32) + summed).astype(jnp.bfloat16)


def solution(mesh):
    fine = Mesh(mesh.devices.reshape(4, 8, 2, 4, 2), ("x", "zl", "zh", "y", "c"))
    dp = ("x", "zl")
    tensor = ("zh", "y", "c")
    in_specs = (
        P(dp + tensor, None),
        P(),
        P(dp, tensor),
        P(dp, tensor),
        P(dp, tensor),
        P(tensor, dp),
    )
    out_specs = P(dp + tensor, None)
    return jax.shard_map(body, mesh=fine, in_specs=in_specs, out_specs=out_specs, check_vma=False)
```

```python
import math

import jax
import jax.numpy as jnp
from jax import lax
from jax.sharding import Mesh, PartitionSpec as P

QH = 32
KVH = 4
HD = 128
SEQ = 128


theta_base = 500000.0
epsilon = 1e-05


def normalize(tokens, norm_gain):
    widened = tokens.astype(jnp.float32)
    mean_square = jnp.mean(widened * widened, axis=-1, keepdims=True)
    return (widened * lax.rsqrt(mean_square + epsilon) * norm_gain[None, :]).astype(jnp.bfloat16)


def head_major(matrix, head_count):
    row_count = matrix.shape[0]
    head_width = matrix.shape[1] // head_count
    return jnp.transpose(matrix.reshape(row_count, head_width, head_count), (0, 2, 1)).reshape(
        row_count, head_count * head_width
    )


def rotary(matrix, head_count, seq_span):
    row_count = matrix.shape[0]
    head_width = matrix.shape[1] // head_count
    half_width = head_width // 2
    position = (jnp.arange(row_count, dtype=jnp.int32) % seq_span).astype(jnp.float32)
    frequency = jnp.exp(
        jnp.arange(half_width, dtype=jnp.float32) * (-2.0 * math.log(theta_base) / head_width)
    )
    angles = position[:, None] * frequency[None, :]
    cosine = jnp.cos(angles)[:, None, :]
    sine_part = jnp.sin(angles)[:, None, :]
    shaped = matrix.reshape(row_count, head_count, head_width)
    first_half = shaped[..., :half_width]
    second_half = shaped[..., half_width:]
    joined = jnp.concatenate(
        [
            first_half * cosine - second_half * sine_part,
            second_half * cosine + first_half * sine_part,
        ],
        axis=-1,
    )
    return joined.reshape(row_count, head_count * head_width)


def attend(queries, key_heads, value_heads, seq_span):
    row_count, head_count, head_width = queries.shape
    seq_count = row_count // seq_span
    query_four = queries.reshape(seq_count, seq_span, head_count, head_width)
    key_four = key_heads.reshape(seq_count, seq_span, head_count, head_width)
    value_four = value_heads.reshape(seq_count, seq_span, head_count, head_width)
    scores = jnp.einsum(
        "nqhd,nkhd->nhqk", query_four, key_four, preferred_element_type=jnp.float32
    ) * (1.0 / math.sqrt(head_width))
    causal = jnp.arange(seq_span)[:, None] >= jnp.arange(seq_span)[None, :]
    raw_weights = jnp.where(causal[None, None], jnp.exp(scores), 0.0)
    weights = (raw_weights / jnp.sum(raw_weights, axis=-1, keepdims=True)).astype(jnp.bfloat16)
    attended = jnp.einsum(
        "nhqk,nkhd->nqhd", weights, value_four, preferred_element_type=jnp.float32
    )
    return attended.astype(jnp.bfloat16).reshape(row_count, head_count * head_width)


def ring_gather(block, axis_name, size):
    if size == 1:
        return block[None]
    index = lax.axis_index(axis_name)
    forward = [(s, (s + 1) % size) for s in range(size)]
    backward = [(s, (s - 1) % size) for s in range(size)]
    relative = [None] * size
    relative[0] = block
    ahead = block
    behind = block
    for step in range(1, size // 2 + 1):
        ahead = lax.ppermute(ahead, axis_name, forward)
        relative[(-step) % size] = ahead
        if step < size - size // 2:
            behind = lax.ppermute(behind, axis_name, backward)
            relative[step] = behind
    stacked = jnp.stack(relative)
    return jnp.roll(stacked, index, axis=0)


def group_gather(block):
    along_zh = ring_gather(block, "zh", 2)
    along_y = ring_gather(along_zh, "y", 4)
    along_c = ring_gather(along_y, "c", 2)
    ordered = jnp.transpose(along_c, (2, 1, 0) + tuple(range(3, along_c.ndim)))
    return ordered.reshape((-1,) + block.shape[1:])


def dp_gather(block, axis):
    return lax.all_gather(lax.all_gather(block, "zl", axis=axis, tiled=True), "x", axis=axis, tiled=True)


def take(array, index, axis):
    return lax.dynamic_index_in_dim(array, index, axis=axis, keepdims=False)


def group_reduce_scatter(partial):
    c_index = lax.axis_index("c")
    y_index = lax.axis_index("y")
    zh_index = lax.axis_index("zh")
    swap = [(0, 1), (1, 0)]
    sent = lax.ppermute(take(partial, 1 - c_index, 2), "c", swap)
    acc = take(partial, c_index, 2).astype(jnp.float32) + sent.astype(jnp.float32)
    mine = take(acc, y_index, 1)
    for shift in range(1, 4):
        outgoing = take(acc, (y_index + shift) % 4, 1).astype(jnp.bfloat16)
        mine = mine + lax.ppermute(outgoing, "y", [(s, (s + shift) % 4) for s in range(4)]).astype(jnp.float32)
    sent = lax.ppermute(take(mine, 1 - zh_index, 0).astype(jnp.bfloat16), "zh", swap)
    return take(mine, zh_index, 0) + sent.astype(jnp.float32)


def body(tokens, norm_gain, w_query, w_key, w_value, w_out):
    tensor_rank = (lax.axis_index("zh") * 4 + lax.axis_index("y")) * 2 + lax.axis_index("c")
    q_cols = w_query.shape[1]
    k_cols = w_key.shape[1]
    stacked = jnp.concatenate([w_query, w_key, w_value], axis=1)
    normed = normalize(tokens, norm_gain)
    stacked, normed = lax.optimization_barrier((stacked, normed))
    payload = jnp.concatenate([stacked, w_out], axis=1)
    along_zl = lax.all_gather(payload, "zl", axis=0, tiled=True)
    in_part = along_zl[:, : stacked.shape[1]]
    out_part = along_zl[:, stacked.shape[1] :].reshape((-1,) + w_out.shape)
    out_part = jnp.transpose(out_part, (1, 0, 2)).reshape(w_out.shape[0], -1)
    in_part, out_part, normed = lax.optimization_barrier((in_part, out_part, normed))
    weights = lax.all_gather(in_part, "x", axis=0, tiled=True)
    weights, out_part = lax.optimization_barrier((weights, out_part))
    out_weights = lax.all_gather(out_part, "x", axis=1, tiled=True)
    gathered = group_gather(normed)
    row_count = gathered.shape[0]
    projected = jnp.dot(gathered, weights, preferred_element_type=jnp.float32)
    query_part = projected[:, :q_cols]
    kv_part = projected[:, q_cols:].astype(jnp.bfloat16)
    kv_all = group_gather(kv_part.T)
    kv_all = kv_all.reshape(-1, 2, k_cols, row_count)
    key_whole = jnp.transpose(kv_all[:, 0], (2, 0, 1)).reshape(row_count, -1).astype(jnp.float32)
    value_whole = jnp.transpose(kv_all[:, 1], (2, 0, 1)).reshape(row_count, -1).astype(jnp.float32)
    local_heads = q_cols // HD
    queries = (
        rotary(query_part, local_heads, SEQ)
        .astype(jnp.bfloat16)
        .reshape(row_count, local_heads, HD)
    )
    key_heads = (
        rotary(head_major(key_whole, KVH), KVH, SEQ)
        .astype(jnp.bfloat16)
        .reshape(row_count, KVH, HD)
    )
    value_heads = head_major(value_whole, KVH).astype(jnp.bfloat16).reshape(row_count, KVH, HD)
    owner = (tensor_rank * local_heads + jnp.arange(local_heads, dtype=jnp.int32)) // (QH // KVH)
    key_heads = jnp.take(key_heads, owner, axis=1)
    value_heads = jnp.take(value_heads, owner, axis=1)
    mixed = attend(queries, key_heads, value_heads, SEQ)
    partial_out = jnp.dot(
        mixed, out_weights, preferred_element_type=jnp.float32
    ).astype(jnp.bfloat16)
    width = partial_out.shape[1]
    blocks = partial_out.reshape(2, 4, 2, row_count // 16, width)
    half = width // 2
    summed = jnp.concatenate(
        [group_reduce_scatter(blocks[..., :half]), group_reduce_scatter(blocks[..., half:])], axis=-1
    )
    return (tokens.astype(jnp.float32) + summed).astype(jnp.bfloat16)


def solution(mesh):
    fine = Mesh(mesh.devices.reshape(4, 8, 2, 4, 2), ("x", "zl", "zh", "y", "c"))
    dp = ("x", "zl")
    tensor = ("zh", "y", "c")
    in_specs = (
        P(dp + tensor, None),
        P(),
        P(dp, tensor),
        P(dp, tensor),
        P(dp, tensor),
        P(tensor, dp),
    )
    out_specs = P(dp + tensor, None)
    return jax.shard_map(body, mesh=fine, in_specs=in_specs, out_specs=out_specs, check_vma=False)
```

```python
import math

import jax
import jax.numpy as jnp
from jax import lax
from jax.sharding import Mesh, PartitionSpec as P

QH = 32
KVH = 4
HD = 128
SEQ = 128


theta_base = 500000.0
epsilon = 1e-05


def normalize(tokens, norm_gain):
    widened = tokens.astype(jnp.float32)
    mean_square = jnp.mean(widened * widened, axis=-1, keepdims=True)
    return (widened * lax.rsqrt(mean_square + epsilon) * norm_gain[None, :]).astype(jnp.bfloat16)


def head_major(matrix, head_count):
    row_count = matrix.shape[0]
    head_width = matrix.shape[1] // head_count
    return jnp.transpose(matrix.reshape(row_count, head_width, head_count), (0, 2, 1)).reshape(
        row_count, head_count * head_width
    )


def rotary(matrix, head_count, seq_span):
    row_count = matrix.shape[0]
    head_width = matrix.shape[1] // head_count
    half_width = head_width // 2
    position = (jnp.arange(row_count, dtype=jnp.int32) % seq_span).astype(jnp.float32)
    frequency = jnp.exp(
        jnp.arange(half_width, dtype=jnp.float32) * (-2.0 * math.log(theta_base) / head_width)
    )
    angles = position[:, None] * frequency[None, :]
    cosine = jnp.cos(angles)[:, None, :]
    sine_part = jnp.sin(angles)[:, None, :]
    shaped = matrix.reshape(row_count, head_count, head_width)
    first_half = shaped[..., :half_width]
    second_half = shaped[..., half_width:]
    joined = jnp.concatenate(
        [
            first_half * cosine - second_half * sine_part,
            second_half * cosine + first_half * sine_part,
        ],
        axis=-1,
    )
    return joined.reshape(row_count, head_count * head_width)


def attend(queries, key_heads, value_heads, seq_span):
    row_count, head_count, head_width = queries.shape
    seq_count = row_count // seq_span
    query_four = queries.reshape(seq_count, seq_span, head_count, head_width)
    key_four = key_heads.reshape(seq_count, seq_span, head_count, head_width)
    value_four = value_heads.reshape(seq_count, seq_span, head_count, head_width)
    scores = jnp.einsum(
        "nqhd,nkhd->nhqk", query_four, key_four, preferred_element_type=jnp.float32
    ) * (1.0 / math.sqrt(head_width))
    causal = jnp.arange(seq_span)[:, None] >= jnp.arange(seq_span)[None, :]
    raw_weights = jnp.where(causal[None, None], jnp.exp(scores), 0.0)
    weights = (raw_weights / jnp.sum(raw_weights, axis=-1, keepdims=True)).astype(jnp.bfloat16)
    attended = jnp.einsum(
        "nhqk,nkhd->nqhd", weights, value_four, preferred_element_type=jnp.float32
    )
    return attended.astype(jnp.bfloat16).reshape(row_count, head_count * head_width)


def ring_gather(block, axis_name, size):
    if size == 1:
        return block[None]
    index = lax.axis_index(axis_name)
    forward = [(s, (s + 1) % size) for s in range(size)]
    backward = [(s, (s - 1) % size) for s in range(size)]
    relative = [None] * size
    relative[0] = block
    ahead = block
    behind = block
    for step in range(1, size // 2 + 1):
        ahead = lax.ppermute(ahead, axis_name, forward)
        relative[(-step) % size] = ahead
        if step < size - size // 2:
            behind = lax.ppermute(behind, axis_name, backward)
            relative[step] = behind
    stacked = jnp.stack(relative)
    return jnp.roll(stacked, index, axis=0)


def group_gather(block):
    along_zh = ring_gather(block, "zh", 2)
    along_y = ring_gather(along_zh, "y", 4)
    along_c = ring_gather(along_y, "c", 2)
    ordered = jnp.transpose(along_c, (2, 1, 0) + tuple(range(3, along_c.ndim)))
    return ordered.reshape((-1,) + block.shape[1:])


def dp_gather(block, axis):
    return lax.all_gather(lax.all_gather(block, "zl", axis=axis, tiled=True), "x", axis=axis, tiled=True)


def take(array, index, axis):
    return lax.dynamic_index_in_dim(array, index, axis=axis, keepdims=False)


def group_reduce_scatter(partial):
    c_index = lax.axis_index("c")
    y_index = lax.axis_index("y")
    zh_index = lax.axis_index("zh")
    swap = [(0, 1), (1, 0)]
    sent = lax.ppermute(take(partial, 1 - c_index, 2), "c", swap)
    acc = take(partial, c_index, 2).astype(jnp.float32) + sent.astype(jnp.float32)
    mine = take(acc, y_index, 1)
    for shift in range(1, 4):
        outgoing = take(acc, (y_index + shift) % 4, 1).astype(jnp.bfloat16)
        mine = mine + lax.ppermute(outgoing, "y", [(s, (s + shift) % 4) for s in range(4)]).astype(jnp.float32)
    sent = lax.ppermute(take(mine, 1 - zh_index, 0).astype(jnp.bfloat16), "zh", swap)
    return take(mine, zh_index, 0) + sent.astype(jnp.float32)


def body(tokens, norm_gain, w_query, w_key, w_value, w_out):
    tensor_rank = (lax.axis_index("zh") * 4 + lax.axis_index("y")) * 2 + lax.axis_index("c")
    q_cols = w_query.shape[1]
    k_cols = w_key.shape[1]
    stacked = jnp.concatenate([w_query, w_key, w_value], axis=1)
    normed = normalize(tokens, norm_gain)
    stacked, normed = lax.optimization_barrier((stacked, normed))
    payload = jnp.concatenate([stacked, w_out], axis=1)
    along_zl = lax.all_gather(payload, "zl", axis=0, tiled=True)
    in_part = along_zl[:, : stacked.shape[1]]
    out_part = along_zl[:, stacked.shape[1] :].reshape((-1,) + w_out.shape)
    out_part = jnp.transpose(out_part, (1, 0, 2)).reshape(w_out.shape[0], -1)
    in_part, out_part, normed = lax.optimization_barrier((in_part, out_part, normed))
    weights = lax.all_gather(in_part, "x", axis=0, tiled=True)
    weights, out_part = lax.optimization_barrier((weights, out_part))
    out_weights = lax.all_gather(out_part, "x", axis=1, tiled=True)
    gathered = group_gather(normed)
    row_count = gathered.shape[0]
    projected = jnp.dot(gathered, weights, preferred_element_type=jnp.float32)
    query_part = projected[:, :q_cols]
    kv_part = projected[:, q_cols:].astype(jnp.bfloat16)
    kv_all = group_gather(kv_part.T)
    kv_all = kv_all.reshape(-1, 2, k_cols, row_count)
    key_whole = jnp.transpose(kv_all[:, 0], (2, 0, 1)).reshape(row_count, -1).astype(jnp.float32)
    value_whole = jnp.transpose(kv_all[:, 1], (2, 0, 1)).reshape(row_count, -1).astype(jnp.float32)
    local_heads = q_cols // HD
    queries = (
        rotary(query_part, local_heads, SEQ)
        .astype(jnp.bfloat16)
        .reshape(row_count, local_heads, HD)
    )
    key_heads = (
        rotary(head_major(key_whole, KVH), KVH, SEQ)
        .astype(jnp.bfloat16)
        .reshape(row_count, KVH, HD)
    )
    value_heads = head_major(value_whole, KVH).astype(jnp.bfloat16).reshape(row_count, KVH, HD)
    owner = (tensor_rank * local_heads + jnp.arange(local_heads, dtype=jnp.int32)) // (QH // KVH)
    key_heads = jnp.take(key_heads, owner, axis=1)
    value_heads = jnp.take(value_heads, owner, axis=1)
    mixed = attend(queries, key_heads, value_heads, SEQ)
    partial_out = jnp.dot(
        mixed, out_weights, preferred_element_type=jnp.float32
    ).astype(jnp.bfloat16)
    width = partial_out.shape[1]
    blocks = partial_out.reshape(2, 4, 2, row_count // 16, width)
    quarter = width // 4
    summed = jnp.concatenate(
        [group_reduce_scatter(blocks[..., k * quarter : (k + 1) * quarter]) for k in range(4)], axis=-1
    )
    return (tokens.astype(jnp.float32) + summed).astype(jnp.bfloat16)


def solution(mesh):
    fine = Mesh(mesh.devices.reshape(4, 8, 2, 4, 2), ("x", "zl", "zh", "y", "c"))
    dp = ("x", "zl")
    tensor = ("zh", "y", "c")
    in_specs = (
        P(dp + tensor, None),
        P(),
        P(dp, tensor),
        P(dp, tensor),
        P(dp, tensor),
        P(tensor, dp),
    )
    out_specs = P(dp + tensor, None)
    return jax.shard_map(body, mesh=fine, in_specs=in_specs, out_specs=out_specs, check_vma=False)
```

```python
import math

import jax
import jax.numpy as jnp
from jax import lax
from jax.sharding import Mesh, PartitionSpec as P

QH = 32
KVH = 4
HD = 128
SEQ = 128


theta_base = 500000.0
epsilon = 1e-05


def normalize(tokens, norm_gain):
    widened = tokens.astype(jnp.float32)
    mean_square = jnp.mean(widened * widened, axis=-1, keepdims=True)
    return (widened * lax.rsqrt(mean_square + epsilon) * norm_gain[None, :]).astype(jnp.bfloat16)


def head_major(matrix, head_count):
    row_count = matrix.shape[0]
    head_width = matrix.shape[1] // head_count
    return jnp.transpose(matrix.reshape(row_count, head_width, head_count), (0, 2, 1)).reshape(
        row_count, head_count * head_width
    )


def rotary(matrix, head_count, seq_span):
    row_count = matrix.shape[0]
    head_width = matrix.shape[1] // head_count
    half_width = head_width // 2
    position = (jnp.arange(row_count, dtype=jnp.int32) % seq_span).astype(jnp.float32)
    frequency = jnp.exp(
        jnp.arange(half_width, dtype=jnp.float32) * (-2.0 * math.log(theta_base) / head_width)
    )
    angles = position[:, None] * frequency[None, :]
    cosine = jnp.cos(angles)[:, None, :]
    sine_part = jnp.sin(angles)[:, None, :]
    shaped = matrix.reshape(row_count, head_count, head_width)
    first_half = shaped[..., :half_width]
    second_half = shaped[..., half_width:]
    joined = jnp.concatenate(
        [
            first_half * cosine - second_half * sine_part,
            second_half * cosine + first_half * sine_part,
        ],
        axis=-1,
    )
    return joined.reshape(row_count, head_count * head_width)


def attend(queries, key_heads, value_heads, seq_span):
    row_count, head_count, head_width = queries.shape
    seq_count = row_count // seq_span
    query_four = queries.reshape(seq_count, seq_span, head_count, head_width)
    key_four = key_heads.reshape(seq_count, seq_span, head_count, head_width)
    value_four = value_heads.reshape(seq_count, seq_span, head_count, head_width)
    scores = jnp.einsum(
        "nqhd,nkhd->nhqk", query_four, key_four, preferred_element_type=jnp.float32
    ) * (1.0 / math.sqrt(head_width))
    causal = jnp.arange(seq_span)[:, None] >= jnp.arange(seq_span)[None, :]
    raw_weights = jnp.where(causal[None, None], jnp.exp(scores), 0.0)
    weights = (raw_weights / jnp.sum(raw_weights, axis=-1, keepdims=True)).astype(jnp.bfloat16)
    attended = jnp.einsum(
        "nhqk,nkhd->nqhd", weights, value_four, preferred_element_type=jnp.float32
    )
    return attended.astype(jnp.bfloat16).reshape(row_count, head_count * head_width)


def ring_gather(block, axis_name, size):
    if size == 1:
        return block[None]
    index = lax.axis_index(axis_name)
    forward = [(s, (s + 1) % size) for s in range(size)]
    backward = [(s, (s - 1) % size) for s in range(size)]
    relative = [None] * size
    relative[0] = block
    ahead = block
    behind = block
    for step in range(1, size // 2 + 1):
        ahead = lax.ppermute(ahead, axis_name, forward)
        relative[(-step) % size] = ahead
        if step < size - size // 2:
            behind = lax.ppermute(behind, axis_name, backward)
            relative[step] = behind
    stacked = jnp.stack(relative)
    return jnp.roll(stacked, index, axis=0)


def group_gather(block, crossed=False):
    along_zh = block if crossed else ring_gather(block, "zh", 2)
    along_y = ring_gather(along_zh, "y", 4)
    along_c = ring_gather(along_y, "c", 2)
    ordered = jnp.transpose(along_c, (2, 1, 0) + tuple(range(3, along_c.ndim)))
    return ordered.reshape((-1,) + along_c.shape[3 + int(crossed):])


def dp_gather(block, axis):
    return lax.all_gather(lax.all_gather(block, "zl", axis=axis, tiled=True), "x", axis=axis, tiled=True)


def take(array, index, axis):
    return lax.dynamic_index_in_dim(array, index, axis=axis, keepdims=False)


def group_reduce_scatter(partial):
    c_index = lax.axis_index("c")
    y_index = lax.axis_index("y")
    zh_index = lax.axis_index("zh")
    swap = [(0, 1), (1, 0)]
    sent = lax.ppermute(take(partial, 1 - c_index, 2), "c", swap)
    acc = take(partial, c_index, 2).astype(jnp.float32) + sent.astype(jnp.float32)
    mine = take(acc, y_index, 1)
    for shift in range(1, 4):
        outgoing = take(acc, (y_index + shift) % 4, 1).astype(jnp.bfloat16)
        mine = mine + lax.ppermute(outgoing, "y", [(s, (s + shift) % 4) for s in range(4)]).astype(jnp.float32)
    sent = lax.ppermute(take(mine, 1 - zh_index, 0).astype(jnp.bfloat16), "zh", swap)
    return take(mine, zh_index, 0) + sent.astype(jnp.float32)


def body(tokens, norm_gain, w_query, w_key, w_value, w_out):
    tensor_rank = (lax.axis_index("zh") * 4 + lax.axis_index("y")) * 2 + lax.axis_index("c")
    q_cols = w_query.shape[1]
    k_cols = w_key.shape[1]
    stacked = jnp.concatenate([w_query, w_key, w_value], axis=1)
    normed = normalize(tokens, norm_gain)
    stacked, normed = lax.optimization_barrier((stacked, normed))
    payload = jnp.concatenate([stacked, w_out], axis=1)
    along_zl = lax.all_gather(payload, "zl", axis=0, tiled=True)
    in_part = along_zl[:, : stacked.shape[1]]
    out_part = along_zl[:, stacked.shape[1] :].reshape((-1,) + w_out.shape)
    out_part = jnp.transpose(out_part, (1, 0, 2)).reshape(w_out.shape[0], -1)
    normed = ring_gather(normed, "zh", 2)
    in_part, out_part, normed = lax.optimization_barrier((in_part, out_part, normed))
    weights = lax.all_gather(in_part, "x", axis=0, tiled=True)
    weights, out_part = lax.optimization_barrier((weights, out_part))
    out_weights = lax.all_gather(out_part, "x", axis=1, tiled=True)
    gathered = group_gather(normed, crossed=True)
    row_count = gathered.shape[0]
    projected = jnp.dot(gathered, weights, preferred_element_type=jnp.float32)
    query_part = projected[:, :q_cols]
    kv_part = projected[:, q_cols:].astype(jnp.bfloat16)
    kv_all = group_gather(kv_part.T)
    kv_all = kv_all.reshape(-1, 2, k_cols, row_count)
    key_whole = jnp.transpose(kv_all[:, 0], (2, 0, 1)).reshape(row_count, -1).astype(jnp.float32)
    value_whole = jnp.transpose(kv_all[:, 1], (2, 0, 1)).reshape(row_count, -1).astype(jnp.float32)
    local_heads = q_cols // HD
    queries = (
        rotary(query_part, local_heads, SEQ)
        .astype(jnp.bfloat16)
        .reshape(row_count, local_heads, HD)
    )
    key_heads = (
        rotary(head_major(key_whole, KVH), KVH, SEQ)
        .astype(jnp.bfloat16)
        .reshape(row_count, KVH, HD)
    )
    value_heads = head_major(value_whole, KVH).astype(jnp.bfloat16).reshape(row_count, KVH, HD)
    owner = (tensor_rank * local_heads + jnp.arange(local_heads, dtype=jnp.int32)) // (QH // KVH)
    key_heads = jnp.take(key_heads, owner, axis=1)
    value_heads = jnp.take(value_heads, owner, axis=1)
    mixed = attend(queries, key_heads, value_heads, SEQ)
    partial_out = jnp.dot(
        mixed, out_weights, preferred_element_type=jnp.float32
    ).astype(jnp.bfloat16)
    width = partial_out.shape[1]
    blocks = partial_out.reshape(2, 4, 2, row_count // 16, width)
    half = width // 2
    summed = jnp.concatenate(
        [group_reduce_scatter(blocks[..., :half]), group_reduce_scatter(blocks[..., half:])], axis=-1
    )
    return (tokens.astype(jnp.float32) + summed).astype(jnp.bfloat16)


def solution(mesh):
    fine = Mesh(mesh.devices.reshape(4, 8, 2, 4, 2), ("x", "zl", "zh", "y", "c"))
    dp = ("x", "zl")
    tensor = ("zh", "y", "c")
    in_specs = (
        P(dp + tensor, None),
        P(),
        P(dp, tensor),
        P(dp, tensor),
        P(dp, tensor),
        P(tensor, dp),
    )
    out_specs = P(dp + tensor, None)
    return jax.shard_map(body, mesh=fine, in_specs=in_specs, out_specs=out_specs, check_vma=False)
```

```python
import math

import jax
import jax.numpy as jnp
from jax import lax
from jax.sharding import Mesh, PartitionSpec as P

QH = 32
KVH = 4
HD = 128
SEQ = 128


theta_base = 500000.0
epsilon = 1e-05


def normalize(tokens, norm_gain):
    widened = tokens.astype(jnp.float32)
    mean_square = jnp.mean(widened * widened, axis=-1, keepdims=True)
    return (widened * lax.rsqrt(mean_square + epsilon) * norm_gain[None, :]).astype(jnp.bfloat16)


def head_major(matrix, head_count):
    row_count = matrix.shape[0]
    head_width = matrix.shape[1] // head_count
    return jnp.transpose(matrix.reshape(row_count, head_width, head_count), (0, 2, 1)).reshape(
        row_count, head_count * head_width
    )


def rotary(matrix, head_count, seq_span):
    row_count = matrix.shape[0]
    head_width = matrix.shape[1] // head_count
    half_width = head_width // 2
    position = (jnp.arange(row_count, dtype=jnp.int32) % seq_span).astype(jnp.float32)
    frequency = jnp.exp(
        jnp.arange(half_width, dtype=jnp.float32) * (-2.0 * math.log(theta_base) / head_width)
    )
    angles = position[:, None] * frequency[None, :]
    cosine = jnp.cos(angles)[:, None, :]
    sine_part = jnp.sin(angles)[:, None, :]
    shaped = matrix.reshape(row_count, head_count, head_width)
    first_half = shaped[..., :half_width]
    second_half = shaped[..., half_width:]
    joined = jnp.concatenate(
        [
            first_half * cosine - second_half * sine_part,
            second_half * cosine + first_half * sine_part,
        ],
        axis=-1,
    )
    return joined.reshape(row_count, head_count * head_width)


def attend(queries, key_heads, value_heads, seq_span):
    row_count, head_count, head_width = queries.shape
    seq_count = row_count // seq_span
    query_four = queries.reshape(seq_count, seq_span, head_count, head_width)
    key_four = key_heads.reshape(seq_count, seq_span, head_count, head_width)
    value_four = value_heads.reshape(seq_count, seq_span, head_count, head_width)
    scores = jnp.einsum(
        "nqhd,nkhd->nhqk", query_four, key_four, preferred_element_type=jnp.float32
    ) * (1.0 / math.sqrt(head_width))
    causal = jnp.arange(seq_span)[:, None] >= jnp.arange(seq_span)[None, :]
    raw_weights = jnp.where(causal[None, None], jnp.exp(scores), 0.0)
    weights = (raw_weights / jnp.sum(raw_weights, axis=-1, keepdims=True)).astype(jnp.bfloat16)
    attended = jnp.einsum(
        "nhqk,nkhd->nqhd", weights, value_four, preferred_element_type=jnp.float32
    )
    return attended.astype(jnp.bfloat16).reshape(row_count, head_count * head_width)


def ring_gather(block, axis_name, size):
    if size == 1:
        return block[None]
    index = lax.axis_index(axis_name)
    forward = [(s, (s + 1) % size) for s in range(size)]
    backward = [(s, (s - 1) % size) for s in range(size)]
    relative = [None] * size
    relative[0] = block
    ahead = block
    behind = block
    for step in range(1, size // 2 + 1):
        ahead = lax.ppermute(ahead, axis_name, forward)
        relative[(-step) % size] = ahead
        if step < size - size // 2:
            behind = lax.ppermute(behind, axis_name, backward)
            relative[step] = behind
    stacked = jnp.stack(relative)
    return jnp.roll(stacked, index, axis=0)


def group_gather(block, crossed=False):
    along_zh = block if crossed else ring_gather(block, "zh", 2)
    along_y = ring_gather(along_zh, "y", 4)
    along_c = ring_gather(along_y, "c", 2)
    ordered = jnp.transpose(along_c, (2, 1, 0) + tuple(range(3, along_c.ndim)))
    return ordered.reshape((-1,) + along_c.shape[3 + int(crossed):])


def dp_gather(block, axis):
    return lax.all_gather(lax.all_gather(block, "zl", axis=axis, tiled=True), "x", axis=axis, tiled=True)


def take(array, index, axis):
    return lax.dynamic_index_in_dim(array, index, axis=axis, keepdims=False)


def group_reduce_scatter(partial):
    c_index = lax.axis_index("c")
    y_index = lax.axis_index("y")
    zh_index = lax.axis_index("zh")
    swap = [(0, 1), (1, 0)]
    sent = lax.ppermute(take(partial, 1 - c_index, 2), "c", swap)
    acc = take(partial, c_index, 2).astype(jnp.float32) + sent.astype(jnp.float32)
    mine = take(acc, y_index, 1)
    for shift in range(1, 4):
        outgoing = take(acc, (y_index + shift) % 4, 1).astype(jnp.bfloat16)
        mine = mine + lax.ppermute(outgoing, "y", [(s, (s + shift) % 4) for s in range(4)]).astype(jnp.float32)
    sent = lax.ppermute(take(mine, 1 - zh_index, 0).astype(jnp.bfloat16), "zh", swap)
    return take(mine, zh_index, 0) + sent.astype(jnp.float32)


def body(tokens, norm_gain, w_query, w_key, w_value, w_out):
    tensor_rank = (lax.axis_index("zh") * 4 + lax.axis_index("y")) * 2 + lax.axis_index("c")
    q_cols = w_query.shape[1]
    k_cols = w_key.shape[1]
    stacked = jnp.concatenate([w_query, w_key, w_value], axis=1)
    normed = normalize(tokens, norm_gain)
    stacked, normed = lax.optimization_barrier((stacked, normed))
    payload = jnp.concatenate([stacked, w_out], axis=1)
    along_zl = lax.all_gather(payload, "zl", axis=0, tiled=True)
    in_part = along_zl[:, : stacked.shape[1]]
    out_part = along_zl[:, stacked.shape[1] :].reshape((-1,) + w_out.shape)
    out_part = jnp.transpose(out_part, (1, 0, 2)).reshape(w_out.shape[0], -1)
    normed = ring_gather(normed, "zh", 2)
    in_part, out_part, normed = lax.optimization_barrier((in_part, out_part, normed))
    weights = lax.all_gather(in_part, "x", axis=0, tiled=True)
    weights, out_part = lax.optimization_barrier((weights, out_part))
    out_weights = lax.all_gather(out_part, "x", axis=1, tiled=True)
    gathered = group_gather(normed, crossed=True)
    row_count = gathered.shape[0]
    kv_part = jnp.dot(gathered, weights[:, q_cols:], preferred_element_type=jnp.float32).astype(jnp.bfloat16)
    kv_part, gathered = lax.optimization_barrier((kv_part, gathered))
    query_part = jnp.dot(gathered, weights[:, :q_cols], preferred_element_type=jnp.float32)
    kv_all = group_gather(kv_part.T)
    kv_all = kv_all.reshape(-1, 2, k_cols, row_count)
    key_whole = jnp.transpose(kv_all[:, 0], (2, 0, 1)).reshape(row_count, -1).astype(jnp.float32)
    value_whole = jnp.transpose(kv_all[:, 1], (2, 0, 1)).reshape(row_count, -1).astype(jnp.float32)
    local_heads = q_cols // HD
    queries = (
        rotary(query_part, local_heads, SEQ)
        .astype(jnp.bfloat16)
        .reshape(row_count, local_heads, HD)
    )
    key_heads = (
        rotary(head_major(key_whole, KVH), KVH, SEQ)
        .astype(jnp.bfloat16)
        .reshape(row_count, KVH, HD)
    )
    value_heads = head_major(value_whole, KVH).astype(jnp.bfloat16).reshape(row_count, KVH, HD)
    owner = (tensor_rank * local_heads + jnp.arange(local_heads, dtype=jnp.int32)) // (QH // KVH)
    key_heads = jnp.take(key_heads, owner, axis=1)
    value_heads = jnp.take(value_heads, owner, axis=1)
    mixed = attend(queries, key_heads, value_heads, SEQ)
    partial_out = jnp.dot(
        mixed, out_weights, preferred_element_type=jnp.float32
    ).astype(jnp.bfloat16)
    width = partial_out.shape[1]
    blocks = partial_out.reshape(2, 4, 2, row_count // 16, width)
    half = width // 2
    summed = jnp.concatenate(
        [group_reduce_scatter(blocks[..., :half]), group_reduce_scatter(blocks[..., half:])], axis=-1
    )
    return (tokens.astype(jnp.float32) + summed).astype(jnp.bfloat16)


def solution(mesh):
    fine = Mesh(mesh.devices.reshape(4, 8, 2, 4, 2), ("x", "zl", "zh", "y", "c"))
    dp = ("x", "zl")
    tensor = ("zh", "y", "c")
    in_specs = (
        P(dp + tensor, None),
        P(),
        P(dp, tensor),
        P(dp, tensor),
        P(dp, tensor),
        P(tensor, dp),
    )
    out_specs = P(dp + tensor, None)
    return jax.shard_map(body, mesh=fine, in_specs=in_specs, out_specs=out_specs, check_vma=False)
```
